256 devices in a mesh: rep: 4 (over y), pipe: 8 (over z_lo, x), tp: 8 (over z_hi, core).
Axes of the slice: x: 4, y: 4, z: 8 (z_hi: 4, z_lo: 2; z = z_hi * 2 + z_lo), core: 2. Of those that a mesh axis runs over, the one named last changes fastest.
Arguments:
- act_forward: bfloat16 [8, 4, 128, 4096], P('pipe', 'rep', 'tp'), may hold values from -6 to 6
- act_saved: bfloat16 [8, 4, 128, 4096], P('pipe', 'rep', 'tp'), may hold values from -6 to 6
- grad_output: bfloat16 [8, 4, 128, 4096], P('pipe', 'rep', 'tp'), may hold values from -6 to 6
- norm_gain: bfloat16 [8, 4096], P('pipe'), may hold values from 0.099609375 to 1.8984375
- up_weight: bfloat16 [8, 4096, 14336], P('pipe', None, ('rep', 'tp')), may hold values from -0.09375 to 0.09375
- down_weight: bfloat16 [8, 14336, 4096], P('pipe', ('rep', 'tp')), may hold values from -0.046875 to 0.046875
- section_layers: int32 [4], replicated, may hold values from 1 to 3, 8 in all
- redirect_count: int32 [3, 4], replicated, may hold values from 0 to 3, as said below
- redirect_dest: int32 [3, 4], replicated, may hold values from 0 to 3, as said below
Outputs:
- arrive_forward: bfloat16 [8, 4, 128, 4096], P('pipe', 'rep', 'tp')
- arrive_backward: bfloat16 [8, 4, 128, 4096], P('pipe', 'rep', 'tp')
The draws below stay inside these ranges and needn't reach their ends.
Inputs may be any that keep to these rules, and one draw needn't show every extreme that they name: `redirect_count`: counts are in blocks of 16 rows. At each boundary every replica either sends to another replica or has count zero; a sender's destination has count zero there, and each replica receives from at most one sender. Following the boundaries in order from 5 live blocks, every replica keeps at least one block and never holds more than 8. At the first boundary every sender sends to the replica 4 / 2 indices away (counted round); one replica sends exactly 3 blocks, filling its receiver to 8, and with four or more replicas another replica sends exactly one block. `redirect_dest`: the destination of a replica with count zero is the replica itself.
All inputs are finite; a program needn't handle non-finite values.
Results may differ from the reference program's by a relative error of at most 0.015.
Values may be sent and summed in bfloat16 or wider, within the bound.
No kernel may reach another device: no remote copies, remote signals or barrier semaphores. Data moves between devices by JAX's collectives and lax.ppermute only.
A program may use at most 128 MiB of HBM per device.

```python
import math
import jax
import jax.numpy as jnp
import numpy as np
from jax import lax

D = 4096
FF = 14336
CAP = 128
BLOCK = 16
MOST_LAYERS = 3
SECTIONS = 4
CAPB = 8
MOST = 3
START = 5
N_REP = 4
N_PIPE = 8
N_TP = 8


def redirect_plan(key):
    base_key = jax.random.fold_in(key, 4049)
    live_blocks = jnp.full((N_REP,), START, jnp.int32)
    count_rows = []
    dest_rows = []
    half_reps = N_REP // 2
    first_start = jax.random.randint(jax.random.fold_in(base_key, 7001), (), 0, N_REP, dtype=jnp.int32)
    lanes = jnp.arange(half_reps, dtype=jnp.int32)
    first_order = jnp.stack([(first_start + lanes) % N_REP, (first_start + lanes + half_reps) % N_REP], axis=1).reshape(N_REP).astype(jnp.int32)
    swapped_index = jnp.arange(N_REP, dtype=jnp.int32) ^ 1
    for boundary in range(SECTIONS - 1):
        step_key = jax.random.fold_in(base_key, boundary)
        if boundary == 0:
            shuffled = first_order
        elif boundary == 1:
            shuffled = jnp.take(first_order, swapped_index)
        else:
            shuffled = jax.random.permutation(jax.random.fold_in(step_key, 0), N_REP).astype(jnp.int32)
        count_row = jnp.zeros((N_REP,), jnp.int32)
        dest_row = jnp.arange(N_REP, dtype=jnp.int32)
        for pair_index in range(N_REP // 2):
            sender = shuffled[2 * pair_index]
            receiver = shuffled[2 * pair_index + 1]
            ceiling = jnp.minimum(jnp.minimum(live_blocks[sender] - 1, CAPB - live_blocks[receiver]), MOST).astype(jnp.int32)
            pair_key = jax.random.fold_in(step_key, pair_index + 1)
            if boundary == 0 and pair_index == 0:
                amount = ceiling
            elif boundary == 0 and pair_index == 1:
                amount = jnp.minimum(ceiling, 1).astype(jnp.int32)
            elif boundary == 1 and pair_index == 0:
                amount = jax.random.randint(pair_key, (), 1, jnp.maximum(ceiling, 1) + 1, dtype=jnp.int32)
                amount = jnp.minimum(amount, ceiling).astype(jnp.int32)
            else:
                amount = jax.random.randint(pair_key, (), 0, ceiling + 1, dtype=jnp.int32)
            count_row = count_row.at[sender].set(amount)
            dest_row = dest_row.at[sender].set(jnp.where(amount > 0, receiver, sender).astype(jnp.int32))
            live_blocks = live_blocks.at[sender].add(-amount).at[receiver].add(amount)
        count_rows.append(count_row)
        dest_rows.append(dest_row)
    return (jnp.stack(count_rows), jnp.stack(dest_rows))


def draw_redirect_count(key, part):
    return redirect_plan(key)[0]


def draw_redirect_dest(key, part):
    return redirect_plan(key)[1]


def block_scale(stream_key, dims, pieces, low, largest):
    loudness, own = 1.0, jax.random.fold_in(stream_key, 6)
    for axis_at, parts in pieces:
        steps = jnp.exp(jax.random.uniform(jax.random.fold_in(own, axis_at), (parts,), jnp.float32, low / len(pieces), largest / len(pieces)))
        loudness = loudness * jnp.repeat(steps, dims[axis_at] // parts).reshape([-1 if axis == axis_at else 1 for axis in range(len(dims))])
    return loudness


def length_profile(count, total, bound, skew):
    portions = [(1 << 20) // math.isqrt(grade ** skew) + 1 for grade in range(2, count + 1)]
    surplus, given = total - bound - (count - 1), [1] * (count - 1)
    while surplus > 0:
        candidates = [i for i in range(count - 1) if given[i] < bound]
        whole, left = sum([portions[i] for i in candidates]), surplus
        for i in candidates:
            extra = min(bound - given[i], max(1, left * portions[i] // whole), surplus)
            given[i] = given[i] + extra
            surplus = surplus - extra
    return np.array([bound] + given)


def ragged(key, count, total, bound, skew):
    if count == 2:
        one = jax.random.randint(key, (), max(1, total - bound), min(bound, total - 1) + 1)
        return jnp.stack([one, total - one])
    sizes = jnp.asarray(length_profile(count, total, bound, skew), jnp.int32)
    pairs = (count - 1) // 2
    giver, taker = sizes[1:1 + 2 * pairs:2], sizes[2:2 + 2 * pairs:2]
    margin = jnp.minimum(giver - 1, bound - taker)
    moved = jax.random.randint(jax.random.fold_in(key, 1), (pairs,), 0, 1 << 20) % (margin + 1)
    sizes = sizes.at[1:1 + 2 * pairs:2].set(giver - moved).at[2:2 + 2 * pairs:2].set(taker + moved)
    return sizes[jax.random.permutation(jax.random.fold_in(key, 2), count)]


def noise(own_key, dims, scale, reach, pieces=(), kind=jnp.bfloat16):
    values = jax.random.normal(own_key, dims, jnp.float32) * scale
    if len(pieces) > 0:
        values = block_scale(own_key, dims, pieces, -0.22, 0.18) * values
    return jnp.clip(values, min=-reach, max=reach).astype(kind)


def setup_inputs(seed: int = 0) -> dict:
    key_list = jax.random.split(jax.random.key(seed), 10)
    return {
        "act_forward": noise(key_list[0], (N_PIPE, N_REP, CAP, D), 1.0, 6.0, ((0, 8), (1, 4), (2, 8))),
        "act_saved": noise(key_list[1], (N_PIPE, N_REP, CAP, D), 1.0, 6.0, ((0, 8), (1, 4), (2, 8))),
        "grad_output": noise(key_list[2], (N_PIPE, N_REP, CAP, D), 1.0, 6.0, ((0, 8), (1, 4), (2, 8))),
        "norm_gain": jnp.clip(1.0 + 0.18 * jax.random.normal(key_list[3], (N_PIPE, D), jnp.float32), 0.099609375, 1.8984375).astype(jnp.bfloat16),
        "up_weight": noise(key_list[4], (N_PIPE, D, FF), D ** -0.5, 0.09375, ((0, 8), (2, 32))),
        "down_weight": noise(key_list[5], (N_PIPE, FF, D), FF ** -0.5, 0.046875, ((0, 8), (1, 32))),
        "section_layers": ragged(key_list[6], SECTIONS, N_PIPE, MOST_LAYERS, 0).astype(jnp.int32),
        "redirect_count": draw_redirect_count(jax.random.fold_in(key_list[9], 71), 0),
        "redirect_dest": draw_redirect_dest(jax.random.fold_in(key_list[9], 71), 0),
    }


EPSILON = 1e-05

def moved_blocks(counts, dests, replica_ids):
    return jnp.where((dests != replica_ids) & (counts > 0), counts, 0).astype(jnp.int32)

def section_plan(section_layers, redirect_count, redirect_dest, segments, replicas):
    replica_ids = jnp.arange(replicas, dtype=jnp.int32)
    section_ends = (jnp.cumsum(section_layers).astype(jnp.int32) - 1)[:-1]
    positions = jnp.arange(segments, dtype=jnp.int32)
    matches = (section_ends[None, :] == positions[:, None]).astype(jnp.int32)
    segment_count = lax.optimization_barrier(jnp.sum(matches[:, :, None] * redirect_count[None, :, :], axis=1)).astype(jnp.int32)
    has_boundary = lax.optimization_barrier(jnp.sum(matches, axis=1)).astype(jnp.int32)[:, None]
    segment_dest = (lax.optimization_barrier(jnp.sum(matches[:, :, None] * redirect_dest[None, :, :], axis=1)).astype(jnp.int32) + (1 - has_boundary) * replica_ids[None, :]).astype(jnp.int32)
    live_list = [jnp.full((replicas,), START, jnp.int32)]
    for position in range(segments - 1):
        moved = moved_blocks(segment_count[position], segment_dest[position], replica_ids)
        incoming = lax.optimization_barrier(jnp.sum(jnp.where(segment_dest[position][:, None] == replica_ids[None, :], moved[:, None], 0), axis=0)).astype(jnp.int32)
        live_list.append((live_list[-1] - moved + incoming).astype(jnp.int32))
    return (jnp.stack(live_list), segment_count, segment_dest)

def source_rows(live_before, counts, dests, replicas):
    replica_ids = jnp.arange(replicas, dtype=jnp.int32)
    block_ids = jnp.arange(CAPB, dtype=jnp.int32)
    moved = moved_blocks(counts, dests, replica_ids)
    sends = moved > 0
    same_dest = (dests[None, :] == dests[:, None]) & (replica_ids[None, :] < replica_ids[:, None]) & sends[None, :]
    kept = (live_before - moved).astype(jnp.int32)
    incoming = lax.optimization_barrier(jnp.sum(jnp.where(sends[:, None] & (dests[:, None] == replica_ids[None, :]), moved[:, None], 0), axis=0)).astype(jnp.int32)
    offset = lax.optimization_barrier(jnp.sum(jnp.where(same_dest, moved[None, :], 0), axis=1)).astype(jnp.int32)
    hits = sends[None, None, :] & (dests[None, None, :] == replica_ids[:, None, None]) & (block_ids[None, :, None] >= offset[None, None, :]) & (block_ids[None, :, None] < (offset + moved)[None, None, :])
    from_block = replica_ids[None, None, :] * CAPB + block_ids[None, :, None] - offset[None, None, :]
    moved_source = lax.optimization_barrier(jnp.sum(jnp.where(hits, from_block, 0), axis=2)).astype(jnp.int32)
    own_local = block_ids[None, :] - incoming[:, None]
    own_ok = (own_local >= 0) & (own_local < kept[:, None])
    own_block = own_local + moved[:, None]
    source_block = jnp.where(jnp.any(hits, axis=2), moved_source, jnp.where(own_ok, replica_ids[:, None] * CAPB + own_block, -1)).astype(jnp.int32)
    row_ids = source_block[:, :, None] * BLOCK + jnp.arange(BLOCK, dtype=jnp.int32)[None, None, :]
    return jnp.where(source_block[:, :, None] >= 0, row_ids, -1).reshape(replicas * CAPB * BLOCK).astype(jnp.int32)

def inverse_rows(source):
    total = source.shape[0]
    target = jnp.where(source >= 0, source, total).astype(jnp.int32)
    return jnp.full((total,), -1, jnp.int32).at[target].set(jnp.arange(total, dtype=jnp.int32), mode='drop')

def pick_rows(values, index):
    taken = jnp.take(values, jnp.maximum(index, 0), axis=0)
    return jnp.where(index[:, None] >= 0, taken, jnp.zeros((), values.dtype))

def normalize(values, gain_row):
    wide = values.astype(jnp.float32)
    scale = lax.rsqrt(lax.optimization_barrier(jnp.mean(wide * wide, axis=-1, keepdims=True)) + EPSILON)
    return (wide * scale * gain_row.astype(jnp.float32)).astype(jnp.bfloat16)

def norm_back(values, gain_row, upstream):
    wide = values.astype(jnp.float32)
    scale = lax.rsqrt(lax.optimization_barrier(jnp.mean(wide * wide, axis=-1, keepdims=True)) + EPSILON)
    weighted = gain_row.astype(jnp.float32) * upstream
    return scale * weighted - wide * (scale * scale * scale) * lax.optimization_barrier(jnp.mean(weighted * wide, axis=-1, keepdims=True))

def silu_slope(upper):
    sigma = jax.nn.sigmoid(upper)
    return sigma * (1.0 + upper * (1.0 - sigma))

def grouped_product(left, right, groups):
    group_width = left.shape[1] // groups

    def add_group(total, group_index):
        first_col = group_index * group_width
        piece = jnp.dot(lax.dynamic_slice_in_dim(left, first_col, group_width, 1), lax.dynamic_slice_in_dim(right, first_col, group_width, 0), preferred_element_type=jnp.float32)
        rounded = lax.optimization_barrier(piece.astype(jnp.bfloat16))
        return (total + rounded.astype(jnp.float32), None)
    total, unused = lax.scan(add_group, jnp.zeros((left.shape[0], right.shape[1]), jnp.float32), jnp.arange(groups, dtype=jnp.int32))
    return total

def reference(act_forward, act_saved, grad_output, norm_gain, up_weight, down_weight, section_layers, redirect_count, redirect_dest):
    segments = N_PIPE
    replicas = N_REP
    groups = N_REP * N_TP
    total_rows = replicas * CAP
    live, segment_count, segment_dest = section_plan(section_layers, redirect_count, redirect_dest, segments, replicas)
    empty = jnp.zeros((replicas, CAP, D), jnp.bfloat16)
    arrive_forward = [empty]
    arrive_backward = []
    for segment_index in range(segments):
        gain_row = norm_gain[segment_index]
        if segment_index < segments - 1:
            fresh = act_forward[segment_index].reshape(total_rows, D)
            hidden = jax.nn.silu(jnp.dot(normalize(fresh, gain_row), up_weight[segment_index], preferred_element_type=jnp.float32)).astype(jnp.bfloat16)
            mixed = grouped_product(hidden, down_weight[segment_index], groups)
            result = (fresh.astype(jnp.float32) + mixed).astype(jnp.bfloat16)
            later = source_rows(live[segment_index], segment_count[segment_index], segment_dest[segment_index], replicas)
            arrive_forward.append(pick_rows(result, later).reshape(replicas, CAP, D))
        if segment_index > 0:
            saved = act_saved[segment_index].reshape(total_rows, D)
            upstream = grad_output[segment_index].reshape(total_rows, D)
            upper = jnp.dot(normalize(saved, gain_row), up_weight[segment_index], preferred_element_type=jnp.float32)
            back_hidden = (jnp.dot(upstream, down_weight[segment_index].T, preferred_element_type=jnp.float32) * silu_slope(upper)).astype(jnp.bfloat16)
            returned = grouped_product(back_hidden, up_weight[segment_index].T, groups)
            gradient = (upstream.astype(jnp.float32) + norm_back(saved, gain_row, returned)).astype(jnp.bfloat16)
            earlier = inverse_rows(source_rows(live[segment_index - 1], segment_count[segment_index - 1], segment_dest[segment_index - 1], replicas))
            arrive_backward.append(pick_rows(gradient, earlier).reshape(replicas, CAP, D))
    arrive_backward.append(empty)
    return (jnp.stack(arrive_forward), jnp.stack(arrive_backward))
```

```python
import jax
import jax.numpy as jnp
from jax import lax
from jax.sharding import PartitionSpec as P

BLOCK = 16
CAPB = 8
START = 5


EPSILON = 1e-05


def from_behind(block, axis, distance):
    devices = range(lax.axis_size(axis))
    route = [(i - distance, i) for i in devices if i - distance in devices]
    return lax.ppermute(block, axis, route)


def moved_blocks(counts, dests, replica_ids):
    return jnp.where((dests != replica_ids) & (counts > 0), counts, 0)


def section_plan(section_layers, redirect_count, redirect_dest, segments, replicas):
    replica_ids = jnp.arange(replicas, dtype=jnp.int32)
    section_ends = (jnp.cumsum(section_layers) - 1)[:-1]
    positions = jnp.arange(segments, dtype=jnp.int32)
    matches = (section_ends[None, :] == positions[:, None]).astype(jnp.int32)
    segment_count = jnp.sum(matches[:, :, None] * redirect_count[None, :, :], axis=1)
    has_boundary = jnp.sum(matches, axis=1)[:, None]
    segment_dest = (
        jnp.sum(matches[:, :, None] * redirect_dest[None, :, :], axis=1)
        + (1 - has_boundary) * replica_ids[None, :]
    )
    live_list = [jnp.full((replicas,), START, jnp.int32)]
    for position in range(segments - 1):
        moved = moved_blocks(segment_count[position], segment_dest[position], replica_ids)
        incoming = jnp.sum(
            jnp.where(segment_dest[position][:, None] == replica_ids[None, :], moved[:, None], 0),
            axis=0,
        )
        live_list.append(live_list[-1] - moved + incoming)
    return (jnp.stack(live_list), segment_count, segment_dest)


def source_rows(live_before, counts, dests, replicas):
    replica_ids = jnp.arange(replicas, dtype=jnp.int32)
    block_ids = jnp.arange(CAPB, dtype=jnp.int32)
    moved = moved_blocks(counts, dests, replica_ids)
    sends = moved > 0
    same_dest = (
        (dests[None, :] == dests[:, None])
        & (replica_ids[None, :] < replica_ids[:, None])
        & sends[None, :]
    )
    kept = live_before - moved
    incoming = jnp.sum(
        jnp.where(sends[:, None] & (dests[:, None] == replica_ids[None, :]), moved[:, None], 0),
        axis=0,
    )
    offset = jnp.sum(jnp.where(same_dest, moved[None, :], 0), axis=1)
    hits = (
        sends[None, None, :]
        & (dests[None, None, :] == replica_ids[:, None, None])
        & (block_ids[None, :, None] >= offset[None, None, :])
        & (block_ids[None, :, None] < (offset + moved)[None, None, :])
    )
    from_block = (
        replica_ids[None, None, :] * CAPB + block_ids[None, :, None] - offset[None, None, :]
    )
    moved_source = jnp.sum(jnp.where(hits, from_block, 0), axis=2)
    own_local = block_ids[None, :] - incoming[:, None]
    own_ok = (own_local >= 0) & (own_local < kept[:, None])
    own_block = own_local + moved[:, None]
    source_block = jnp.where(
        jnp.any(hits, axis=2),
        moved_source,
        jnp.where(own_ok, replica_ids[:, None] * CAPB + own_block, -1),
    )
    row_ids = source_block[:, :, None] * BLOCK + jnp.arange(BLOCK, dtype=jnp.int32)[None, None, :]
    return jnp.where(source_block[:, :, None] >= 0, row_ids, -1).reshape(replicas * CAPB * BLOCK)


def inverse_rows(source):
    total = source.shape[0]
    target = jnp.where(source >= 0, source, total)
    return (
        jnp.full((total,), -1, jnp.int32)
        .at[target]
        .set(jnp.arange(total, dtype=jnp.int32), mode="drop")
    )


def normalize(values, gain_row):
    wide = values.astype(jnp.float32)
    scale = lax.rsqrt(jnp.mean(wide * wide, axis=-1, keepdims=True) + EPSILON)
    return (wide * scale * gain_row.astype(jnp.float32)).astype(jnp.bfloat16)


def norm_back(values, gain_row, upstream):
    wide = values.astype(jnp.float32)
    scale = lax.rsqrt(jnp.mean(wide * wide, axis=-1, keepdims=True) + EPSILON)
    weighted = gain_row.astype(jnp.float32) * upstream
    return scale * weighted - wide * (scale * scale * scale) * jnp.mean(
        weighted * wide, axis=-1, keepdims=True
    )


def silu_slope(upper):
    sigma = jax.nn.sigmoid(upper)
    return sigma * (1.0 + upper * (1.0 - sigma))


def against_rows(left, right):
    return lax.dot_general(
        left, right, (((1,), (1,)), ((), ())), preferred_element_type=jnp.float32
    )


def pick_blocks(values, blocks):
    shaped = values.reshape(blocks.shape[0], BLOCK, values.shape[-1])
    taken = jnp.take(shaped, jnp.maximum(blocks, 0), axis=0)
    kept = jnp.where(blocks[:, None, None] >= 0, taken, jnp.zeros((), values.dtype))
    return kept.reshape(values.shape)


def row_blocks(rows):
    heads = rows[::BLOCK]
    return jnp.where(heads >= 0, heads // BLOCK, -1)


def local(
    act_forward,
    act_saved,
    grad_output,
    norm_gain,
    up_weight,
    down_weight,
    section_layers,
    redirect_count,
    redirect_dest,
):
    segments = lax.axis_size("pipe")
    replicas = lax.axis_size("rep")
    splits = lax.axis_size("tp")
    segment_index = lax.axis_index("pipe")
    replica_index = lax.axis_index("rep")
    split_index = lax.axis_index("tp")
    local_rows = act_forward.shape[2]
    gain_row = norm_gain[0]
    w_up = up_weight[0]
    w_down = down_weight[0]
    live, segment_count, segment_dest = section_plan(
        section_layers, redirect_count, redirect_dest, segments, replicas
    )
    prior = jnp.maximum(segment_index - 1, 0)
    later = row_blocks(
        source_rows(
            live[segment_index], segment_count[segment_index], segment_dest[segment_index], replicas
        )
    )
    earlier = row_blocks(
        inverse_rows(source_rows(live[prior], segment_count[prior], segment_dest[prior], replicas))
    )
    my_offset = (replica_index * splits + split_index) * local_rows
    own = jnp.stack([act_forward[0, 0], act_saved[0, 0], grad_output[0, 0]])
    every = lax.all_gather(own, ("rep", "tp"), axis=1, tiled=True)
    fresh = pick_blocks(every[0], later)
    saved = pick_blocks(every[1], earlier)
    upstream = pick_blocks(every[2], earlier)
    hidden = jax.nn.silu(
        jnp.dot(normalize(fresh, gain_row), w_up, preferred_element_type=jnp.float32)
    ).astype(jnp.bfloat16)
    upper = jnp.dot(normalize(saved, gain_row), w_up, preferred_element_type=jnp.float32)
    back_hidden = (against_rows(upstream, w_down) * silu_slope(upper)).astype(jnp.bfloat16)
    mixed = lax.psum_scatter(
        jnp.dot(hidden, w_down, preferred_element_type=jnp.float32).astype(jnp.bfloat16),
        ("rep", "tp"),
        scatter_dimension=0,
        tiled=True,
    ).astype(jnp.float32)
    returned = lax.psum_scatter(
        against_rows(back_hidden, w_up).astype(jnp.bfloat16),
        ("rep", "tp"),
        scatter_dimension=0,
        tiled=True,
    ).astype(jnp.float32)
    fresh_mine = lax.dynamic_slice_in_dim(fresh, my_offset, local_rows)
    saved_mine = lax.dynamic_slice_in_dim(saved, my_offset, local_rows)
    upstream_mine = lax.dynamic_slice_in_dim(upstream, my_offset, local_rows)
    result = (fresh_mine.astype(jnp.float32) + mixed).astype(jnp.bfloat16)
    gradient = (
        upstream_mine.astype(jnp.float32) + norm_back(saved_mine, gain_row, returned)
    ).astype(jnp.bfloat16)
    arrive_forward = from_behind(result, "pipe", 1)
    arrive_backward = from_behind(gradient, "pipe", -1)
    return (arrive_forward[None, None], arrive_backward[None, None])


def solution(mesh):
    in_specs = (
        P("pipe", "rep", "tp", None),
        P("pipe", "rep", "tp", None),
        P("pipe", "rep", "tp", None),
        P("pipe", None),
        P("pipe", None, ("rep", "tp")),
        P("pipe", ("rep", "tp"), None),
        P(),
        P(),
        P(),
    )
    out_specs = (P("pipe", "rep", "tp", None), P("pipe", "rep", "tp", None))
    return jax.shard_map(local, mesh=mesh, in_specs=in_specs, out_specs=out_specs, check_vma=False)
```

```python
import jax
import jax.numpy as jnp
from jax import lax
from jax.sharding import Mesh, PartitionSpec as P

BLOCK = 16
CAPB = 8
START = 5


EPSILON = 1e-05


def from_behind(block, axis, distance):
    devices = range(lax.axis_size(axis))
    route = [(i - distance, i) for i in devices if i - distance in devices]
    return lax.ppermute(block, axis, route)


def moved_blocks(counts, dests, replica_ids):
    return jnp.where((dests != replica_ids) & (counts > 0), counts, 0)


def section_plan(section_layers, redirect_count, redirect_dest, segments, replicas):
    replica_ids = jnp.arange(replicas, dtype=jnp.int32)
    section_ends = (jnp.cumsum(section_layers) - 1)[:-1]
    positions = jnp.arange(segments, dtype=jnp.int32)
    matches = (section_ends[None, :] == positions[:, None]).astype(jnp.int32)
    segment_count = jnp.sum(matches[:, :, None] * redirect_count[None, :, :], axis=1)
    has_boundary = jnp.sum(matches, axis=1)[:, None]
    segment_dest = (
        jnp.sum(matches[:, :, None] * redirect_dest[None, :, :], axis=1)
        + (1 - has_boundary) * replica_ids[None, :]
    )
    live_list = [jnp.full((replicas,), START, jnp.int32)]
    for position in range(segments - 1):
        moved = moved_blocks(segment_count[position], segment_dest[position], replica_ids)
        incoming = jnp.sum(
            jnp.where(segment_dest[position][:, None] == replica_ids[None, :], moved[:, None], 0),
            axis=0,
        )
        live_list.append(live_list[-1] - moved + incoming)
    return (jnp.stack(live_list), segment_count, segment_dest)


def source_rows(live_before, counts, dests, replicas):
    replica_ids = jnp.arange(replicas, dtype=jnp.int32)
    block_ids = jnp.arange(CAPB, dtype=jnp.int32)
    moved = moved_blocks(counts, dests, replica_ids)
    sends = moved > 0
    same_dest = (
        (dests[None, :] == dests[:, None])
        & (replica_ids[None, :] < replica_ids[:, None])
        & sends[None, :]
    )
    kept = live_before - moved
    incoming = jnp.sum(
        jnp.where(sends[:, None] & (dests[:, None] == replica_ids[None, :]), moved[:, None], 0),
        axis=0,
    )
    offset = jnp.sum(jnp.where(same_dest, moved[None, :], 0), axis=1)
    hits = (
        sends[None, None, :]
        & (dests[None, None, :] == replica_ids[:, None, None])
        & (block_ids[None, :, None] >= offset[None, None, :])
        & (block_ids[None, :, None] < (offset + moved)[None, None, :])
    )
    from_block = (
        replica_ids[None, None, :] * CAPB + block_ids[None, :, None] - offset[None, None, :]
    )
    moved_source = jnp.sum(jnp.where(hits, from_block, 0), axis=2)
    own_local = block_ids[None, :] - incoming[:, None]
    own_ok = (own_local >= 0) & (own_local < kept[:, None])
    own_block = own_local + moved[:, None]
    source_block = jnp.where(
        jnp.any(hits, axis=2),
        moved_source,
        jnp.where(own_ok, replica_ids[:, None] * CAPB + own_block, -1),
    )
    row_ids = source_block[:, :, None] * BLOCK + jnp.arange(BLOCK, dtype=jnp.int32)[None, None, :]
    return jnp.where(source_block[:, :, None] >= 0, row_ids, -1).reshape(replicas * CAPB * BLOCK)


def inverse_rows(source):
    total = source.shape[0]
    target = jnp.where(source >= 0, source, total)
    return (
        jnp.full((total,), -1, jnp.int32)
        .at[target]
        .set(jnp.arange(total, dtype=jnp.int32), mode="drop")
    )


def normalize(values, gain_row):
    wide = values.astype(jnp.float32)
    scale = lax.rsqrt(jnp.mean(wide * wide, axis=-1, keepdims=True) + EPSILON)
    return (wide * scale * gain_row.astype(jnp.float32)).astype(jnp.bfloat16)


def norm_back(values, gain_row, upstream):
    wide = values.astype(jnp.float32)
    scale = lax.rsqrt(jnp.mean(wide * wide, axis=-1, keepdims=True) + EPSILON)
    weighted = gain_row.astype(jnp.float32) * upstream
    return scale * weighted - wide * (scale * scale * scale) * jnp.mean(
        weighted * wide, axis=-1, keepdims=True
    )


def silu_slope(upper):
    sigma = jax.nn.sigmoid(upper)
    return sigma * (1.0 + upper * (1.0 - sigma))


def against_rows(left, right):
    return lax.dot_general(
        left, right, (((1,), (1,)), ((), ())), preferred_element_type=jnp.float32
    )


def pick_blocks(values, blocks):
    shaped = values.reshape(-1, BLOCK, values.shape[-1])
    taken = jnp.take(shaped, jnp.maximum(blocks, 0), axis=0)
    kept = jnp.where(blocks[:, None, None] >= 0, taken, jnp.zeros((), values.dtype))
    return kept.reshape(-1, values.shape[-1])


def row_blocks(rows):
    heads = rows[::BLOCK]
    return jnp.where(heads >= 0, heads // BLOCK, -1)


def swap_cores(values):
    return lax.ppermute(values, "core", [(0, 1), (1, 0)])


def gathered_place(blocks, cores, core_index, per_core):
    split = blocks % (cores * per_core)
    spot = (split % cores != core_index) * (lax.axis_size("rep") * per_core)
    spot = spot + (blocks // (cores * per_core)) * per_core + split // cores
    return jnp.where(blocks >= 0, spot, -1)


def two_stage_sum(partial, half):
    mine, theirs = partial[:half], partial[half:]
    total = (mine.astype(jnp.float32) + swap_cores(theirs).astype(jnp.float32)).astype(jnp.bfloat16)
    return lax.psum_scatter(total, ("rep", "zh"), scatter_dimension=0, tiled=True).astype(
        jnp.float32
    )


def local(
    act_forward,
    act_saved,
    grad_output,
    norm_gain,
    up_weight,
    down_weight,
    section_layers,
    redirect_count,
    redirect_dest,
):
    segments = lax.axis_size("pipe")
    replicas = lax.axis_size("rep")
    per_core = lax.axis_size("zh")
    cores = lax.axis_size("core")
    segment_index = lax.axis_index("pipe")
    replica_index = lax.axis_index("rep")
    zh_index = lax.axis_index("zh")
    core_index = lax.axis_index("core")
    local_rows = act_forward.shape[2]
    gain_row = norm_gain[0]
    w_up = up_weight[0]
    w_down = down_weight[0]
    live, segment_count, segment_dest = section_plan(
        section_layers, redirect_count, redirect_dest, segments, replicas
    )
    prior = jnp.maximum(segment_index - 1, 0)
    later = row_blocks(
        source_rows(
            live[segment_index], segment_count[segment_index], segment_dest[segment_index], replicas
        )
    )
    earlier = row_blocks(
        inverse_rows(source_rows(live[prior], segment_count[prior], segment_dest[prior], replicas))
    )
    group = replicas * per_core
    slots = jnp.arange(cores * group, dtype=jnp.int32)
    slot_core = jnp.where(slots < group, core_index, cores - 1 - core_index)
    slot_group = slots % group
    dest = (slot_group // per_core) * (per_core * cores) + (slot_group % per_core) * cores + slot_core
    me = replica_index * (per_core * cores) + zh_index * cores + core_index
    later_at = gathered_place(later, cores, core_index, per_core)
    earlier_at = gathered_place(earlier, cores, core_index, per_core)
    own = jnp.stack([act_forward[0, 0], act_saved[0, 0], grad_output[0, 0]])
    near = lax.all_gather(own, ("rep", "zh"), axis=1, tiled=True)
    every = jnp.concatenate([near, swap_cores(near)], axis=1)
    hidden = jax.nn.silu(
        jnp.dot(normalize(every[0], gain_row), w_up, preferred_element_type=jnp.float32)
    ).astype(jnp.bfloat16)
    upper = jnp.dot(normalize(every[1], gain_row), w_up, preferred_element_type=jnp.float32)
    back_hidden = (against_rows(every[2], w_down) * silu_slope(upper)).astype(jnp.bfloat16)
    half = group * local_rows
    mixed = two_stage_sum(
        jnp.dot(pick_blocks(hidden, later_at[dest]), w_down, preferred_element_type=jnp.float32).astype(
            jnp.bfloat16
        ),
        half,
    )
    returned = two_stage_sum(
        against_rows(pick_blocks(back_hidden, earlier_at[dest]), w_up).astype(jnp.bfloat16), half
    )
    fresh_mine = pick_blocks(every[0], later_at[me][None])
    saved_mine = pick_blocks(every[1], earlier_at[me][None])
    upstream_mine = pick_blocks(every[2], earlier_at[me][None])
    result = (fresh_mine.astype(jnp.float32) + mixed).astype(jnp.bfloat16)
    gradient = (
        upstream_mine.astype(jnp.float32) + norm_back(saved_mine, gain_row, returned)
    ).astype(jnp.bfloat16)
    arrive_forward = from_behind(result, "pipe", 1)
    arrive_backward = from_behind(gradient, "pipe", -1)
    return (arrive_forward[None, None], arrive_backward[None, None])


def solution(mesh):
    cores = 2
    shape = mesh.devices.shape
    fine = Mesh(
        mesh.devices.reshape(shape[0], shape[1], shape[2] // cores, cores),
        ("rep", "pipe", "zh", "core"),
    )
    rows = P("pipe", "rep", ("zh", "core"), None)
    in_specs = (
        rows,
        rows,
        rows,
        P("pipe", None),
        P("pipe", None, ("rep", "zh", "core")),
        P("pipe", ("rep", "zh", "core"), None),
        P(),
        P(),
        P(),
    )
    out_specs = (rows, rows)
    return jax.shard_map(local, mesh=fine, in_specs=in_specs, out_specs=out_specs, check_vma=False)
```

```python
import jax
import jax.numpy as jnp
from jax import lax
from jax.sharding import Mesh, PartitionSpec as P

BLOCK = 16
CAPB = 8
START = 5


EPSILON = 1e-05


def from_behind(block, axis, distance):
    devices = range(lax.axis_size(axis))
    route = [(i - distance, i) for i in devices if i - distance in devices]
    return lax.ppermute(block, axis, route)


def moved_blocks(counts, dests, replica_ids):
    return jnp.where((dests != replica_ids) & (counts > 0), counts, 0)


def section_plan(section_layers, redirect_count, redirect_dest, segments, replicas):
    replica_ids = jnp.arange(replicas, dtype=jnp.int32)
    section_ends = (jnp.cumsum(section_layers) - 1)[:-1]
    positions = jnp.arange(segments, dtype=jnp.int32)
    matches = (section_ends[None, :] == positions[:, None]).astype(jnp.int32)
    segment_count = jnp.sum(matches[:, :, None] * redirect_count[None, :, :], axis=1)
    has_boundary = jnp.sum(matches, axis=1)[:, None]
    segment_dest = (
        jnp.sum(matches[:, :, None] * redirect_dest[None, :, :], axis=1)
        + (1 - has_boundary) * replica_ids[None, :]
    )
    live_list = [jnp.full((replicas,), START, jnp.int32)]
    for position in range(segments - 1):
        moved = moved_blocks(segment_count[position], segment_dest[position], replica_ids)
        incoming = jnp.sum(
            jnp.where(segment_dest[position][:, None] == replica_ids[None, :], moved[:, None], 0),
            axis=0,
        )
        live_list.append(live_list[-1] - moved + incoming)
    return (jnp.stack(live_list), segment_count, segment_dest)


def source_rows(live_before, counts, dests, replicas):
    replica_ids = jnp.arange(replicas, dtype=jnp.int32)
    block_ids = jnp.arange(CAPB, dtype=jnp.int32)
    moved = moved_blocks(counts, dests, replica_ids)
    sends = moved > 0
    same_dest = (
        (dests[None, :] == dests[:, None])
        & (replica_ids[None, :] < replica_ids[:, None])
        & sends[None, :]
    )
    kept = live_before - moved
    incoming = jnp.sum(
        jnp.where(sends[:, None] & (dests[:, None] == replica_ids[None, :]), moved[:, None], 0),
        axis=0,
    )
    offset = jnp.sum(jnp.where(same_dest, moved[None, :], 0), axis=1)
    hits = (
        sends[None, None, :]
        & (dests[None, None, :] == replica_ids[:, None, None])
        & (block_ids[None, :, None] >= offset[None, None, :])
        & (block_ids[None, :, None] < (offset + moved)[None, None, :])
    )
    from_block = (
        replica_ids[None, None, :] * CAPB + block_ids[None, :, None] - offset[None, None, :]
    )
    moved_source = jnp.sum(jnp.where(hits, from_block, 0), axis=2)
    own_local = block_ids[None, :] - incoming[:, None]
    own_ok = (own_local >= 0) & (own_local < kept[:, None])
    own_block = own_local + moved[:, None]
    source_block = jnp.where(
        jnp.any(hits, axis=2),
        moved_source,
        jnp.where(own_ok, replica_ids[:, None] * CAPB + own_block, -1),
    )
    row_ids = source_block[:, :, None] * BLOCK + jnp.arange(BLOCK, dtype=jnp.int32)[None, None, :]
    return jnp.where(source_block[:, :, None] >= 0, row_ids, -1).reshape(replicas * CAPB * BLOCK)


def inverse_rows(source):
    total = source.shape[0]
    target = jnp.where(source >= 0, source, total)
    return (
        jnp.full((total,), -1, jnp.int32)
        .at[target]
        .set(jnp.arange(total, dtype=jnp.int32), mode="drop")
    )


def normalize(values, gain_row):
    wide = values.astype(jnp.float32)
    scale = lax.rsqrt(jnp.mean(wide * wide, axis=-1, keepdims=True) + EPSILON)
    return (wide * scale * gain_row.astype(jnp.float32)).astype(jnp.bfloat16)


def norm_back(values, gain_row, upstream):
    wide = values.astype(jnp.float32)
    scale = lax.rsqrt(jnp.mean(wide * wide, axis=-1, keepdims=True) + EPSILON)
    weighted = gain_row.astype(jnp.float32) * upstream
    return scale * weighted - wide * (scale * scale * scale) * jnp.mean(
        weighted * wide, axis=-1, keepdims=True
    )


def silu_slope(upper):
    sigma = jax.nn.sigmoid(upper)
    return sigma * (1.0 + upper * (1.0 - sigma))


def against_rows(left, right):
    return lax.dot_general(
        left, right, (((1,), (1,)), ((), ())), preferred_element_type=jnp.float32
    )


def pick_blocks(values, blocks):
    shaped = values.reshape(-1, BLOCK, values.shape[-1])
    taken = jnp.take(shaped, jnp.maximum(blocks, 0), axis=0)
    kept = jnp.where(blocks[:, None, None] >= 0, taken, jnp.zeros((), values.dtype))
    return kept.reshape(-1, values.shape[-1])


def row_blocks(rows):
    heads = rows[::BLOCK]
    return jnp.where(heads >= 0, heads // BLOCK, -1)


def swap_cores(values):
    return lax.ppermute(values, "core", [(0, 1), (1, 0)])


def shift(values, axis, step):
    size = lax.axis_size(axis)
    return lax.ppermute(values, axis, [(i, (i + step) % size) for i in range(size)])


def ring_gather(values, axis):
    half = values.shape[-2] // 2
    from_left = shift(values, axis, 1)
    from_right = shift(values, axis, -1)
    first = shift(from_left[..., :half, :], axis, 1)
    second = shift(from_right[..., half:, :], axis, -1)
    far = jnp.concatenate([first, second], axis=-2)
    return jnp.stack([values, from_right, far, from_left])


def ring_scatter(parts, axis):
    half = parts.shape[-2] // 2
    far = parts[2].astype(jnp.bfloat16)
    from_left = shift(far[..., :half, :], axis, 1).astype(jnp.float32)
    from_right = shift(far[..., half:, :], axis, -1).astype(jnp.float32)
    up = jnp.concatenate([parts[1][..., :half, :] + from_left, parts[1][..., half:, :]], axis=-2)
    down = jnp.concatenate([parts[3][..., :half, :], parts[3][..., half:, :] + from_right], axis=-2)
    return (
        parts[0]
        + shift(up.astype(jnp.bfloat16), axis, 1).astype(jnp.float32)
        + shift(down.astype(jnp.bfloat16), axis, -1).astype(jnp.float32)
    )


def gather_rows(values):
    near = ring_gather(ring_gather(values[None], "zh")[:, 0], "rep")
    both = jnp.stack([near, swap_cores(near)])
    return both.reshape(-1, values.shape[-1])


def scatter_rows(partial):
    rows, width = BLOCK, partial.shape[-1]
    shaped = partial.reshape(2, lax.axis_size("rep"), lax.axis_size("zh"), rows, width)
    total = shaped[0].astype(jnp.float32) + swap_cores(shaped[1]).astype(jnp.float32)
    return ring_scatter(ring_scatter(total, "rep"), "zh")


def gathered_place(blocks, replica_index, zh_index, core_index):
    replicas, per_core, cores = lax.axis_size("rep"), lax.axis_size("zh"), lax.axis_size("core")
    split = blocks % (cores * per_core)
    spot = (split % cores != core_index) * (replicas * per_core)
    spot = spot + ((blocks // (cores * per_core) - replica_index) % replicas) * per_core
    spot = spot + (split // cores - zh_index) % per_core
    return jnp.where(blocks >= 0, spot, -1)


def local(
    act_forward,
    act_saved,
    grad_output,
    norm_gain,
    up_weight,
    down_weight,
    section_layers,
    redirect_count,
    redirect_dest,
):
    segments = lax.axis_size("pipe")
    replicas = lax.axis_size("rep")
    per_core = lax.axis_size("zh")
    cores = lax.axis_size("core")
    segment_index = lax.axis_index("pipe")
    replica_index = lax.axis_index("rep")
    zh_index = lax.axis_index("zh")
    core_index = lax.axis_index("core")
    local_rows = act_forward.shape[2]
    gain_row = norm_gain[0]
    w_up = up_weight[0]
    w_down = down_weight[0]
    live, segment_count, segment_dest = section_plan(
        section_layers, redirect_count, redirect_dest, segments, replicas
    )
    prior = jnp.maximum(segment_index - 1, 0)
    later = row_blocks(
        source_rows(
            live[segment_index], segment_count[segment_index], segment_dest[segment_index], replicas
        )
    )
    earlier = row_blocks(
        inverse_rows(source_rows(live[prior], segment_count[prior], segment_dest[prior], replicas))
    )
    group = replicas * per_core
    slots = jnp.arange(cores * group, dtype=jnp.int32)
    slot_core = jnp.where(slots < group, core_index, cores - 1 - core_index)
    slot_rep = (replica_index + (slots % group) // per_core) % replicas
    slot_zh = (zh_index + slots % per_core) % per_core
    dest = slot_rep * (per_core * cores) + slot_zh * cores + slot_core
    me = replica_index * (per_core * cores) + zh_index * cores + core_index
    later_at = gathered_place(later, replica_index, zh_index, core_index)
    earlier_at = gathered_place(earlier, replica_index, zh_index, core_index)
    every = [gather_rows(part[0, 0]) for part in (act_forward, act_saved, grad_output)]
    hidden = jax.nn.silu(
        jnp.dot(normalize(every[0], gain_row), w_up, preferred_element_type=jnp.float32)
    ).astype(jnp.bfloat16)
    upper = jnp.dot(normalize(every[1], gain_row), w_up, preferred_element_type=jnp.float32)
    back_hidden = (against_rows(every[2], w_down) * silu_slope(upper)).astype(jnp.bfloat16)
    mixed = scatter_rows(
        jnp.dot(pick_blocks(hidden, later_at[dest]), w_down, preferred_element_type=jnp.float32).astype(
            jnp.bfloat16
        )
    )
    returned = scatter_rows(
        against_rows(pick_blocks(back_hidden, earlier_at[dest]), w_up).astype(jnp.bfloat16)
    )
    fresh_mine = pick_blocks(every[0], later_at[me][None])
    saved_mine = pick_blocks(every[1], earlier_at[me][None])
    upstream_mine = pick_blocks(every[2], earlier_at[me][None])
    result = (fresh_mine.astype(jnp.float32) + mixed).astype(jnp.bfloat16)
    gradient = (
        upstream_mine.astype(jnp.float32) + norm_back(saved_mine, gain_row, returned)
    ).astype(jnp.bfloat16)
    arrive_forward = from_behind(result, "pipe", 1)
    arrive_backward = from_behind(gradient, "pipe", -1)
    return (arrive_forward[None, None], arrive_backward[None, None])


def solution(mesh):
    cores = 2
    shape = mesh.devices.shape
    fine = Mesh(
        mesh.devices.reshape(shape[0], shape[1], shape[2] // cores, cores),
        ("rep", "pipe", "zh", "core"),
    )
    rows = P("pipe", "rep", ("zh", "core"), None)
    in_specs = (
        rows,
        rows,
        rows,
        P("pipe", None),
        P("pipe", None, ("rep", "zh", "core")),
        P("pipe", ("rep", "zh", "core"), None),
        P(),
        P(),
        P(),
    )
    out_specs = (rows, rows)
    return jax.shard_map(local, mesh=fine, in_specs=in_specs, out_specs=out_specs, check_vma=False)
```

```python
import jax
import jax.numpy as jnp
from jax import lax
from jax.sharding import Mesh, PartitionSpec as P

BLOCK = 16
CAPB = 8
START = 5


EPSILON = 1e-05


def from_behind(block, axis, distance):
    devices = range(lax.axis_size(axis))
    route = [(i - distance, i) for i in devices if i - distance in devices]
    return lax.ppermute(block, axis, route)


def moved_blocks(counts, dests, replica_ids):
    return jnp.where((dests != replica_ids) & (counts > 0), counts, 0)


def section_plan(section_layers, redirect_count, redirect_dest, segments, replicas):
    replica_ids = jnp.arange(replicas, dtype=jnp.int32)
    section_ends = (jnp.cumsum(section_layers) - 1)[:-1]
    positions = jnp.arange(segments, dtype=jnp.int32)
    matches = (section_ends[None, :] == positions[:, None]).astype(jnp.int32)
    segment_count = jnp.sum(matches[:, :, None] * redirect_count[None, :, :], axis=1)
    has_boundary = jnp.sum(matches, axis=1)[:, None]
    segment_dest = (
        jnp.sum(matches[:, :, None] * redirect_dest[None, :, :], axis=1)
        + (1 - has_boundary) * replica_ids[None, :]
    )
    live_list = [jnp.full((replicas,), START, jnp.int32)]
    for position in range(segments - 1):
        moved = moved_blocks(segment_count[position], segment_dest[position], replica_ids)
        incoming = jnp.sum(
            jnp.where(segment_dest[position][:, None] == replica_ids[None, :], moved[:, None], 0),
            axis=0,
        )
        live_list.append(live_list[-1] - moved + incoming)
    return (jnp.stack(live_list), segment_count, segment_dest)


def source_rows(live_before, counts, dests, replicas):
    replica_ids = jnp.arange(replicas, dtype=jnp.int32)
    block_ids = jnp.arange(CAPB, dtype=jnp.int32)
    moved = moved_blocks(counts, dests, replica_ids)
    sends = moved > 0
    same_dest = (
        (dests[None, :] == dests[:, None])
        & (replica_ids[None, :] < replica_ids[:, None])
        & sends[None, :]
    )
    kept = live_before - moved
    incoming = jnp.sum(
        jnp.where(sends[:, None] & (dests[:, None] == replica_ids[None, :]), moved[:, None], 0),
        axis=0,
    )
    offset = jnp.sum(jnp.where(same_dest, moved[None, :], 0), axis=1)
    hits = (
        sends[None, None, :]
        & (dests[None, None, :] == replica_ids[:, None, None])
        & (block_ids[None, :, None] >= offset[None, None, :])
        & (block_ids[None, :, None] < (offset + moved)[None, None, :])
    )
    from_block = (
        replica_ids[None, None, :] * CAPB + block_ids[None, :, None] - offset[None, None, :]
    )
    moved_source = jnp.sum(jnp.where(hits, from_block, 0), axis=2)
    own_local = block_ids[None, :] - incoming[:, None]
    own_ok = (own_local >= 0) & (own_local < kept[:, None])
    own_block = own_local + moved[:, None]
    source_block = jnp.where(
        jnp.any(hits, axis=2),
        moved_source,
        jnp.where(own_ok, replica_ids[:, None] * CAPB + own_block, -1),
    )
    row_ids = source_block[:, :, None] * BLOCK + jnp.arange(BLOCK, dtype=jnp.int32)[None, None, :]
    return jnp.where(source_block[:, :, None] >= 0, row_ids, -1).reshape(replicas * CAPB * BLOCK)


def inverse_rows(source):
    total = source.shape[0]
    target = jnp.where(source >= 0, source, total)
    return (
        jnp.full((total,), -1, jnp.int32)
        .at[target]
        .set(jnp.arange(total, dtype=jnp.int32), mode="drop")
    )


def normalize(values, gain_row):
    wide = values.astype(jnp.float32)
    scale = lax.rsqrt(jnp.mean(wide * wide, axis=-1, keepdims=True) + EPSILON)
    return (wide * scale * gain_row.astype(jnp.float32)).astype(jnp.bfloat16)


def norm_back(values, gain_row, upstream):
    wide = values.astype(jnp.float32)
    scale = lax.rsqrt(jnp.mean(wide * wide, axis=-1, keepdims=True) + EPSILON)
    weighted = gain_row.astype(jnp.float32) * upstream
    return scale * weighted - wide * (scale * scale * scale) * jnp.mean(
        weighted * wide, axis=-1, keepdims=True
    )


def silu_slope(upper):
    sigma = jax.nn.sigmoid(upper)
    return sigma * (1.0 + upper * (1.0 - sigma))


def against_rows(left, right):
    return lax.dot_general(
        left, right, (((1,), (1,)), ((), ())), preferred_element_type=jnp.float32
    )


def pick_blocks(values, blocks):
    shaped = values.reshape(-1, BLOCK, values.shape[-1])
    taken = jnp.take(shaped, jnp.maximum(blocks, 0), axis=0)
    kept = jnp.where(blocks[:, None, None] >= 0, taken, jnp.zeros((), values.dtype))
    return kept.reshape(-1, values.shape[-1])


def row_blocks(rows):
    heads = rows[::BLOCK]
    return jnp.where(heads >= 0, heads // BLOCK, -1)


def swap_cores(values):
    return lax.ppermute(values, "core", [(0, 1), (1, 0)])


def shift(values, axis, step):
    size = lax.axis_size(axis)
    return lax.ppermute(values, axis, [(i, (i + step) % size) for i in range(size)])


def ring_gather(values, axis):
    half = values.shape[-2] // 2
    from_left = shift(values, axis, 1)
    from_right = shift(values, axis, -1)
    first = shift(from_left[..., :half, :], axis, 1)
    second = shift(from_right[..., half:, :], axis, -1)
    far = jnp.concatenate([first, second], axis=-2)
    return jnp.stack([values, from_right, far, from_left], axis=1)


def ring_scatter(parts, axis):
    half = parts.shape[-2] // 2
    far = parts[:, 2].astype(jnp.bfloat16)
    from_left = shift(far[..., :half, :], axis, 1).astype(jnp.float32)
    from_right = shift(far[..., half:, :], axis, -1).astype(jnp.float32)
    near_up, near_down = parts[:, 1], parts[:, 3]
    up = jnp.concatenate([near_up[..., :half, :] + from_left, near_up[..., half:, :]], axis=-2)
    down = jnp.concatenate([near_down[..., :half, :], near_down[..., half:, :] + from_right], axis=-2)
    return (
        parts[:, 0]
        + shift(up.astype(jnp.bfloat16), axis, 1).astype(jnp.float32)
        + shift(down.astype(jnp.bfloat16), axis, -1).astype(jnp.float32)
    )


def gather_rows(values):
    near = ring_gather(ring_gather(values, "zh"), "rep")
    both = jnp.stack([near, swap_cores(near)], axis=1)
    return both.reshape(values.shape[0], -1, values.shape[-1])


def scatter_rows(partial):
    width = partial.shape[-1]
    shaped = partial.reshape(
        partial.shape[0], 2, lax.axis_size("rep"), lax.axis_size("zh"), BLOCK, width
    )
    total = shaped[:, 0].astype(jnp.float32) + swap_cores(shaped[:, 1]).astype(jnp.float32)
    return ring_scatter(ring_scatter(total, "rep"), "zh")


def gathered_place(blocks, replica_index, zh_index, core_index):
    replicas, per_core, cores = lax.axis_size("rep"), lax.axis_size("zh"), lax.axis_size("core")
    split = blocks % (cores * per_core)
    spot = (split % cores != core_index) * (replicas * per_core)
    spot = spot + ((blocks // (cores * per_core) - replica_index) % replicas) * per_core
    spot = spot + (split // cores - zh_index) % per_core
    return jnp.where(blocks >= 0, spot, -1)


def local(
    act_forward,
    act_saved,
    grad_output,
    norm_gain,
    up_weight,
    down_weight,
    section_layers,
    redirect_count,
    redirect_dest,
):
    segments = lax.axis_size("pipe")
    replicas = lax.axis_size("rep")
    per_core = lax.axis_size("zh")
    cores = lax.axis_size("core")
    segment_index = lax.axis_index("pipe")
    replica_index = lax.axis_index("rep")
    zh_index = lax.axis_index("zh")
    core_index = lax.axis_index("core")
    local_rows = act_forward.shape[2]
    gain_row = norm_gain[0]
    w_up = up_weight[0]
    w_down = down_weight[0]
    live, segment_count, segment_dest = section_plan(
        section_layers, redirect_count, redirect_dest, segments, replicas
    )
    prior = jnp.maximum(segment_index - 1, 0)
    later = row_blocks(
        source_rows(
            live[segment_index], segment_count[segment_index], segment_dest[segment_index], replicas
        )
    )
    earlier = row_blocks(
        inverse_rows(source_rows(live[prior], segment_count[prior], segment_dest[prior], replicas))
    )
    group = replicas * per_core
    slots = jnp.arange(cores * group, dtype=jnp.int32)
    slot_core = jnp.where(slots < group, core_index, cores - 1 - core_index)
    slot_rep = (replica_index + (slots % group) // per_core) % replicas
    slot_zh = (zh_index + slots % per_core) % per_core
    dest = slot_rep * (per_core * cores) + slot_zh * cores + slot_core
    me = replica_index * (per_core * cores) + zh_index * cores + core_index
    later_at = gathered_place(later, replica_index, zh_index, core_index)
    earlier_at = gathered_place(earlier, replica_index, zh_index, core_index)
    every = gather_rows(jnp.stack([act_forward[0, 0], act_saved[0, 0], grad_output[0, 0]]))
    hidden = jax.nn.silu(
        jnp.dot(normalize(every[0], gain_row), w_up, preferred_element_type=jnp.float32)
    ).astype(jnp.bfloat16)
    upper = jnp.dot(normalize(every[1], gain_row), w_up, preferred_element_type=jnp.float32)
    back_hidden = (against_rows(every[2], w_down) * silu_slope(upper)).astype(jnp.bfloat16)
    mixed, returned = scatter_rows(
        jnp.stack(
            [
                jnp.dot(
                    pick_blocks(hidden, later_at[dest]), w_down, preferred_element_type=jnp.float32
                ).astype(jnp.bfloat16),
                against_rows(pick_blocks(back_hidden, earlier_at[dest]), w_up).astype(jnp.bfloat16),
            ]
        )
    )
    fresh_mine = pick_blocks(every[0], later_at[me][None])
    saved_mine = pick_blocks(every[1], earlier_at[me][None])
    upstream_mine = pick_blocks(every[2], earlier_at[me][None])
    result = (fresh_mine.astype(jnp.float32) + mixed).astype(jnp.bfloat16)
    gradient = (
        upstream_mine.astype(jnp.float32) + norm_back(saved_mine, gain_row, returned)
    ).astype(jnp.bfloat16)
    arrive_forward = from_behind(result, "pipe", 1)
    arrive_backward = from_behind(gradient, "pipe", -1)
    return (arrive_forward[None, None], arrive_backward[None, None])


def solution(mesh):
    cores = 2
    shape = mesh.devices.shape
    fine = Mesh(
        mesh.devices.reshape(shape[0], shape[1], shape[2] // cores, cores),
        ("rep", "pipe", "zh", "core"),
    )
    rows = P("pipe", "rep", ("zh", "core"), None)
    in_specs = (
        rows,
        rows,
        rows,
        P("pipe", None),
        P("pipe", None, ("rep", "zh", "core")),
        P("pipe", ("rep", "zh", "core"), None),
        P(),
        P(),
        P(),
    )
    out_specs = (rows, rows)
    return jax.shard_map(local, mesh=fine, in_specs=in_specs, out_specs=out_specs, check_vma=False)
```

```python
import jax
import jax.numpy as jnp
from jax import lax
from jax.sharding import Mesh, PartitionSpec as P

BLOCK = 16
CAPB = 8
START = 5


EPSILON = 1e-05


def from_behind(block, axis, distance):
    devices = range(lax.axis_size(axis))
    route = [(i - distance, i) for i in devices if i - distance in devices]
    return lax.ppermute(block, axis, route)


def moved_blocks(counts, dests, replica_ids):
    return jnp.where((dests != replica_ids) & (counts > 0), counts, 0)


def section_plan(section_layers, redirect_count, redirect_dest, segments, replicas):
    replica_ids = jnp.arange(replicas, dtype=jnp.int32)
    section_ends = (jnp.cumsum(section_layers) - 1)[:-1]
    positions = jnp.arange(segments, dtype=jnp.int32)
    matches = (section_ends[None, :] == positions[:, None]).astype(jnp.int32)
    segment_count = jnp.sum(matches[:, :, None] * redirect_count[None, :, :], axis=1)
    has_boundary = jnp.sum(matches, axis=1)[:, None]
    segment_dest = (
        jnp.sum(matches[:, :, None] * redirect_dest[None, :, :], axis=1)
        + (1 - has_boundary) * replica_ids[None, :]
    )
    live_list = [jnp.full((replicas,), START, jnp.int32)]
    for position in range(segments - 1):
        moved = moved_blocks(segment_count[position], segment_dest[position], replica_ids)
        incoming = jnp.sum(
            jnp.where(segment_dest[position][:, None] == replica_ids[None, :], moved[:, None], 0),
            axis=0,
        )
        live_list.append(live_list[-1] - moved + incoming)
    return (jnp.stack(live_list), segment_count, segment_dest)


def source_rows(live_before, counts, dests, replicas):
    replica_ids = jnp.arange(replicas, dtype=jnp.int32)
    block_ids = jnp.arange(CAPB, dtype=jnp.int32)
    moved = moved_blocks(counts, dests, replica_ids)
    sends = moved > 0
    same_dest = (
        (dests[None, :] == dests[:, None])
        & (replica_ids[None, :] < replica_ids[:, None])
        & sends[None, :]
    )
    kept = live_before - moved
    incoming = jnp.sum(
        jnp.where(sends[:, None] & (dests[:, None] == replica_ids[None, :]), moved[:, None], 0),
        axis=0,
    )
    offset = jnp.sum(jnp.where(same_dest, moved[None, :], 0), axis=1)
    hits = (
        sends[None, None, :]
        & (dests[None, None, :] == replica_ids[:, None, None])
        & (block_ids[None, :, None] >= offset[None, None, :])
        & (block_ids[None, :, None] < (offset + moved)[None, None, :])
    )
    from_block = (
        replica_ids[None, None, :] * CAPB + block_ids[None, :, None] - offset[None, None, :]
    )
    moved_source = jnp.sum(jnp.where(hits, from_block, 0), axis=2)
    own_local = block_ids[None, :] - incoming[:, None]
    own_ok = (own_local >= 0) & (own_local < kept[:, None])
    own_block = own_local + moved[:, None]
    source_block = jnp.where(
        jnp.any(hits, axis=2),
        moved_source,
        jnp.where(own_ok, replica_ids[:, None] * CAPB + own_block, -1),
    )
    row_ids = source_block[:, :, None] * BLOCK + jnp.arange(BLOCK, dtype=jnp.int32)[None, None, :]
    return jnp.where(source_block[:, :, None] >= 0, row_ids, -1).reshape(replicas * CAPB * BLOCK)


def inverse_rows(source):
    total = source.shape[0]
    target = jnp.where(source >= 0, source, total)
    return (
        jnp.full((total,), -1, jnp.int32)
        .at[target]
        .set(jnp.arange(total, dtype=jnp.int32), mode="drop")
    )


def normalize(values, gain_row):
    wide = values.astype(jnp.float32)
    scale = lax.rsqrt(jnp.mean(wide * wide, axis=-1, keepdims=True) + EPSILON)
    return (wide * scale * gain_row.astype(jnp.float32)).astype(jnp.bfloat16)


def norm_back(values, gain_row, upstream):
    wide = values.astype(jnp.float32)
    scale = lax.rsqrt(jnp.mean(wide * wide, axis=-1, keepdims=True) + EPSILON)
    weighted = gain_row.astype(jnp.float32) * upstream
    return scale * weighted - wide * (scale * scale * scale) * jnp.mean(
        weighted * wide, axis=-1, keepdims=True
    )


def silu_slope(upper):
    sigma = jax.nn.sigmoid(upper)
    return sigma * (1.0 + upper * (1.0 - sigma))


def against_rows(left, right):
    return lax.dot_general(
        left, right, (((1,), (1,)), ((), ())), preferred_element_type=jnp.float32
    )


def pick_blocks(values, blocks):
    shaped = values.reshape(-1, BLOCK, values.shape[-1])
    taken = jnp.take(shaped, jnp.maximum(blocks, 0), axis=0)
    kept = jnp.where(blocks[:, None, None] >= 0, taken, jnp.zeros((), values.dtype))
    return kept.reshape(-1, values.shape[-1])


def row_blocks(rows):
    heads = rows[::BLOCK]
    return jnp.where(heads >= 0, heads // BLOCK, -1)


def swap_cores(values):
    return lax.ppermute(values, "core", [(0, 1), (1, 0)])


def shift(values, axis, step):
    size = lax.axis_size(axis)
    return lax.ppermute(values, axis, [(i, (i + step) % size) for i in range(size)])


def ring_gather(values, axis):
    half = values.shape[-2] // 2
    from_left = shift(values, axis, 1)
    from_right = shift(values, axis, -1)
    first = shift(from_left[..., :half, :], axis, 1)
    second = shift(from_right[..., half:, :], axis, -1)
    far = jnp.concatenate([first, second], axis=-2)
    return jnp.stack([values, from_right, far, from_left], axis=1)


def ring_scatter(parts, axis):
    half = parts.shape[-2] // 2
    far = parts[:, 2].astype(jnp.bfloat16)
    from_left = shift(far[..., :half, :], axis, 1).astype(jnp.float32)
    from_right = shift(far[..., half:, :], axis, -1).astype(jnp.float32)
    near_up, near_down = parts[:, 1], parts[:, 3]
    up = jnp.concatenate([near_up[..., :half, :] + from_left, near_up[..., half:, :]], axis=-2)
    down = jnp.concatenate([near_down[..., :half, :], near_down[..., half:, :] + from_right], axis=-2)
    return (
        parts[:, 0]
        + shift(up.astype(jnp.bfloat16), axis, 1).astype(jnp.float32)
        + shift(down.astype(jnp.bfloat16), axis, -1).astype(jnp.float32)
    )


def gather_rows(values):
    near = ring_gather(ring_gather(values, "zh"), "rep")
    both = jnp.stack([near, swap_cores(near)], axis=1)
    return both.reshape(values.shape[0], -1, values.shape[-1])


def scatter_rows(partial):
    width = partial.shape[-1]
    shaped = partial.reshape(
        partial.shape[0], 2, lax.axis_size("rep"), lax.axis_size("zh"), BLOCK, width
    )
    total = shaped[:, 0].astype(jnp.float32) + swap_cores(shaped[:, 1]).astype(jnp.float32)
    return ring_scatter(ring_scatter(total, "rep"), "zh")


def gathered_place(blocks, replica_index, zh_index, core_index):
    replicas, per_core, cores = lax.axis_size("rep"), lax.axis_size("zh"), lax.axis_size("core")
    split = blocks % (cores * per_core)
    spot = (split % cores != core_index) * (replicas * per_core)
    spot = spot + ((blocks // (cores * per_core) - replica_index) % replicas) * per_core
    spot = spot + (split // cores - zh_index) % per_core
    return jnp.where(blocks >= 0, spot, -1)


def local(
    act_forward,
    act_saved,
    grad_output,
    norm_gain,
    up_weight,
    down_weight,
    section_layers,
    redirect_count,
    redirect_dest,
):
    segments = lax.axis_size("pipe")
    replicas = lax.axis_size("rep")
    per_core = lax.axis_size("zh")
    cores = lax.axis_size("core")
    segment_index = lax.axis_index("pipe")
    replica_index = lax.axis_index("rep")
    zh_index = lax.axis_index("zh")
    core_index = lax.axis_index("core")
    local_rows = act_forward.shape[2]
    gain_row = norm_gain[0]
    w_up = up_weight[0]
    w_down = down_weight[0]
    live, segment_count, segment_dest = section_plan(
        section_layers, redirect_count, redirect_dest, segments, replicas
    )
    prior = jnp.maximum(segment_index - 1, 0)
    later = row_blocks(
        source_rows(
            live[segment_index], segment_count[segment_index], segment_dest[segment_index], replicas
        )
    )
    earlier = row_blocks(
        inverse_rows(source_rows(live[prior], segment_count[prior], segment_dest[prior], replicas))
    )
    group = replicas * per_core
    slots = jnp.arange(cores * group, dtype=jnp.int32)
    slot_core = jnp.where(slots < group, core_index, cores - 1 - core_index)
    slot_rep = (replica_index + (slots % group) // per_core) % replicas
    slot_zh = (zh_index + slots % per_core) % per_core
    dest = slot_rep * (per_core * cores) + slot_zh * cores + slot_core
    me = replica_index * (per_core * cores) + zh_index * cores + core_index
    later_at = gathered_place(later, replica_index, zh_index, core_index)
    earlier_at = gathered_place(earlier, replica_index, zh_index, core_index)
    fresh_every = gather_rows(act_forward[0])
    saved_every, upstream_every = gather_rows(jnp.stack([act_saved[0, 0], grad_output[0, 0]]))
    every = (fresh_every[0], saved_every, upstream_every)
    hidden = jax.nn.silu(
        jnp.dot(normalize(every[0], gain_row), w_up, preferred_element_type=jnp.float32)
    ).astype(jnp.bfloat16)
    upper = jnp.dot(normalize(every[1], gain_row), w_up, preferred_element_type=jnp.float32)
    back_hidden = (against_rows(every[2], w_down) * silu_slope(upper)).astype(jnp.bfloat16)
    mixed = scatter_rows(
        jnp.dot(pick_blocks(hidden, later_at[dest]), w_down, preferred_element_type=jnp.float32).astype(
            jnp.bfloat16
        )[None]
    )[0]
    returned = scatter_rows(
        against_rows(pick_blocks(back_hidden, earlier_at[dest]), w_up).astype(jnp.bfloat16)[None]
    )[0]
    fresh_mine = pick_blocks(every[0], later_at[me][None])
    saved_mine = pick_blocks(every[1], earlier_at[me][None])
    upstream_mine = pick_blocks(every[2], earlier_at[me][None])
    result = (fresh_mine.astype(jnp.float32) + mixed).astype(jnp.bfloat16)
    gradient = (
        upstream_mine.astype(jnp.float32) + norm_back(saved_mine, gain_row, returned)
    ).astype(jnp.bfloat16)
    arrive_forward = from_behind(result, "pipe", 1)
    arrive_backward = from_behind(gradient, "pipe", -1)
    return (arrive_forward[None, None], arrive_backward[None, None])


def solution(mesh):
    cores = 2
    shape = mesh.devices.shape
    fine = Mesh(
        mesh.devices.reshape(shape[0], shape[1], shape[2] // cores, cores),
        ("rep", "pipe", "zh", "core"),
    )
    rows = P("pipe", "rep", ("zh", "core"), None)
    in_specs = (
        rows,
        rows,
        rows,
        P("pipe", None),
        P("pipe", None, ("rep", "zh", "core")),
        P("pipe", ("rep", "zh", "core"), None),
        P(),
        P(),
        P(),
    )
    out_specs = (rows, rows)
    return jax.shard_map(local, mesh=fine, in_specs=in_specs, out_specs=out_specs, check_vma=False)
```

```python
import jax
import jax.numpy as jnp
from jax import lax
from jax.sharding import Mesh, PartitionSpec as P

BLOCK = 16
CAPB = 8
START = 5


EPSILON = 1e-05


def from_behind(block, axis, distance):
    devices = range(lax.axis_size(axis))
    route = [(i - distance, i) for i in devices if i - distance in devices]
    return lax.ppermute(block, axis, route)


def moved_blocks(counts, dests, replica_ids):
    return jnp.where((dests != replica_ids) & (counts > 0), counts, 0)


def section_plan(section_layers, redirect_count, redirect_dest, segments, replicas):
    replica_ids = jnp.arange(replicas, dtype=jnp.int32)
    section_ends = (jnp.cumsum(section_layers) - 1)[:-1]
    positions = jnp.arange(segments, dtype=jnp.int32)
    matches = (section_ends[None, :] == positions[:, None]).astype(jnp.int32)
    segment_count = jnp.sum(matches[:, :, None] * redirect_count[None, :, :], axis=1)
    has_boundary = jnp.sum(matches, axis=1)[:, None]
    segment_dest = (
        jnp.sum(matches[:, :, None] * redirect_dest[None, :, :], axis=1)
        + (1 - has_boundary) * replica_ids[None, :]
    )
    live_list = [jnp.full((replicas,), START, jnp.int32)]
    for position in range(segments - 1):
        moved = moved_blocks(segment_count[position], segment_dest[position], replica_ids)
        incoming = jnp.sum(
            jnp.where(segment_dest[position][:, None] == replica_ids[None, :], moved[:, None], 0),
            axis=0,
        )
        live_list.append(live_list[-1] - moved + incoming)
    return (jnp.stack(live_list), segment_count, segment_dest)


def source_rows(live_before, counts, dests, replicas):
    replica_ids = jnp.arange(replicas, dtype=jnp.int32)
    block_ids = jnp.arange(CAPB, dtype=jnp.int32)
    moved = moved_blocks(counts, dests, replica_ids)
    sends = moved > 0
    same_dest = (
        (dests[None, :] == dests[:, None])
        & (replica_ids[None, :] < replica_ids[:, None])
        & sends[None, :]
    )
    kept = live_before - moved
    incoming = jnp.sum(
        jnp.where(sends[:, None] & (dests[:, None] == replica_ids[None, :]), moved[:, None], 0),
        axis=0,
    )
    offset = jnp.sum(jnp.where(same_dest, moved[None, :], 0), axis=1)
    hits = (
        sends[None, None, :]
        & (dests[None, None, :] == replica_ids[:, None, None])
        & (block_ids[None, :, None] >= offset[None, None, :])
        & (block_ids[None, :, None] < (offset + moved)[None, None, :])
    )
    from_block = (
        replica_ids[None, None, :] * CAPB + block_ids[None, :, None] - offset[None, None, :]
    )
    moved_source = jnp.sum(jnp.where(hits, from_block, 0), axis=2)
    own_local = block_ids[None, :] - incoming[:, None]
    own_ok = (own_local >= 0) & (own_local < kept[:, None])
    own_block = own_local + moved[:, None]
    source_block = jnp.where(
        jnp.any(hits, axis=2),
        moved_source,
        jnp.where(own_ok, replica_ids[:, None] * CAPB + own_block, -1),
    )
    row_ids = source_block[:, :, None] * BLOCK + jnp.arange(BLOCK, dtype=jnp.int32)[None, None, :]
    return jnp.where(source_block[:, :, None] >= 0, row_ids, -1).reshape(replicas * CAPB * BLOCK)


def inverse_rows(source):
    total = source.shape[0]
    target = jnp.where(source >= 0, source, total)
    return (
        jnp.full((total,), -1, jnp.int32)
        .at[target]
        .set(jnp.arange(total, dtype=jnp.int32), mode="drop")
    )


def normalize(values, gain_row):
    wide = values.astype(jnp.float32)
    scale = lax.rsqrt(jnp.mean(wide * wide, axis=-1, keepdims=True) + EPSILON)
    return (wide * scale * gain_row.astype(jnp.float32)).astype(jnp.bfloat16)


def norm_back(values, gain_row, upstream):
    wide = values.astype(jnp.float32)
    scale = lax.rsqrt(jnp.mean(wide * wide, axis=-1, keepdims=True) + EPSILON)
    weighted = gain_row.astype(jnp.float32) * upstream
    return scale * weighted - wide * (scale * scale * scale) * jnp.mean(
        weighted * wide, axis=-1, keepdims=True
    )


def silu_slope(upper):
    sigma = jax.nn.sigmoid(upper)
    return sigma * (1.0 + upper * (1.0 - sigma))


def against_rows(left, right):
    return lax.dot_general(
        left, right, (((1,), (1,)), ((), ())), preferred_element_type=jnp.float32
    )


def pick_blocks(values, blocks):
    shaped = values.reshape(-1, BLOCK, values.shape[-1])
    taken = jnp.take(shaped, jnp.maximum(blocks, 0), axis=0)
    kept = jnp.where(blocks[:, None, None] >= 0, taken, jnp.zeros((), values.dtype))
    return kept.reshape(-1, values.shape[-1])


def row_blocks(rows):
    heads = rows[::BLOCK]
    return jnp.where(heads >= 0, heads // BLOCK, -1)


def swap_cores(values):
    return lax.ppermute(values, "core", [(0, 1), (1, 0)])


def shift(values, axis, step):
    size = lax.axis_size(axis)
    return lax.ppermute(values, axis, [(i, (i + step) % size) for i in range(size)])


def ring_gather(values, axis):
    half = values.shape[-2] // 2
    from_left = shift(values, axis, 1)
    from_right = shift(values, axis, -1)
    first = shift(from_left[..., :half, :], axis, 1)
    second = shift(from_right[..., half:, :], axis, -1)
    far = jnp.concatenate([first, second], axis=-2)
    return jnp.stack([values, from_right, far, from_left], axis=1)


def ring_scatter(parts, axis):
    half = parts.shape[-2] // 2
    far = parts[:, 2].astype(jnp.bfloat16)
    from_left = shift(far[..., :half, :], axis, 1).astype(jnp.float32)
    from_right = shift(far[..., half:, :], axis, -1).astype(jnp.float32)
    near_up, near_down = parts[:, 1], parts[:, 3]
    up = jnp.concatenate([near_up[..., :half, :] + from_left, near_up[..., half:, :]], axis=-2)
    down = jnp.concatenate([near_down[..., :half, :], near_down[..., half:, :] + from_right], axis=-2)
    return (
        parts[:, 0]
        + shift(up.astype(jnp.bfloat16), axis, 1).astype(jnp.float32)
        + shift(down.astype(jnp.bfloat16), axis, -1).astype(jnp.float32)
    )


def gather_rows(values):
    near = ring_gather(ring_gather(values, "zh"), "rep")
    both = jnp.stack([near, swap_cores(near)], axis=1)
    return both.reshape(values.shape[0], -1, values.shape[-1])


def scatter_rows(partial):
    width = partial.shape[-1]
    shaped = partial.reshape(
        partial.shape[0], 2, lax.axis_size("rep"), lax.axis_size("zh"), BLOCK, width
    )
    total = shaped[:, 0].astype(jnp.float32) + swap_cores(shaped[:, 1]).astype(jnp.float32)
    return ring_scatter(ring_scatter(total, "rep"), "zh")


def gathered_place(blocks, replica_index, zh_index, core_index):
    replicas, per_core, cores = lax.axis_size("rep"), lax.axis_size("zh"), lax.axis_size("core")
    split = blocks % (cores * per_core)
    spot = (split % cores != core_index) * (replicas * per_core)
    spot = spot + ((blocks // (cores * per_core) - replica_index) % replicas) * per_core
    spot = spot + (split // cores - zh_index) % per_core
    return jnp.where(blocks >= 0, spot, -1)


def local(
    act_forward,
    act_saved,
    grad_output,
    norm_gain,
    up_weight,
    down_weight,
    section_layers,
    redirect_count,
    redirect_dest,
):
    segments = lax.axis_size("pipe")
    replicas = lax.axis_size("rep")
    per_core = lax.axis_size("zh")
    cores = lax.axis_size("core")
    segment_index = lax.axis_index("pipe")
    replica_index = lax.axis_index("rep")
    zh_index = lax.axis_index("zh")
    core_index = lax.axis_index("core")
    local_rows = act_forward.shape[2]
    gain_row = norm_gain[0]
    w_up = up_weight[0]
    w_down = down_weight[0]
    live, segment_count, segment_dest = section_plan(
        section_layers, redirect_count, redirect_dest, segments, replicas
    )
    prior = jnp.maximum(segment_index - 1, 0)
    later = row_blocks(
        source_rows(
            live[segment_index], segment_count[segment_index], segment_dest[segment_index], replicas
        )
    )
    earlier = row_blocks(
        inverse_rows(source_rows(live[prior], segment_count[prior], segment_dest[prior], replicas))
    )
    group = replicas * per_core
    slots = jnp.arange(cores * group, dtype=jnp.int32)
    slot_core = jnp.where(slots < group, core_index, cores - 1 - core_index)
    slot_rep = (replica_index + (slots % group) // per_core) % replicas
    slot_zh = (zh_index + slots % per_core) % per_core
    dest = slot_rep * (per_core * cores) + slot_zh * cores + slot_core
    me = replica_index * (per_core * cores) + zh_index * cores + core_index
    later_at = gathered_place(later, replica_index, zh_index, core_index)
    earlier_at = gathered_place(earlier, replica_index, zh_index, core_index)
    fresh_every = gather_rows(act_forward[0])
    pair, fresh_every = lax.optimization_barrier(
        (jnp.stack([act_saved[0, 0], grad_output[0, 0]]), fresh_every)
    )
    saved_every, upstream_every = gather_rows(pair)
    every = (fresh_every[0], saved_every, upstream_every)
    hidden = jax.nn.silu(
        jnp.dot(normalize(every[0], gain_row), w_up, preferred_element_type=jnp.float32)
    ).astype(jnp.bfloat16)
    upper = jnp.dot(normalize(every[1], gain_row), w_up, preferred_element_type=jnp.float32)
    back_hidden = (against_rows(every[2], w_down) * silu_slope(upper)).astype(jnp.bfloat16)
    mixed = scatter_rows(
        jnp.dot(pick_blocks(hidden, later_at[dest]), w_down, preferred_element_type=jnp.float32).astype(
            jnp.bfloat16
        )[None]
    )[0]
    returned = scatter_rows(
        against_rows(pick_blocks(back_hidden, earlier_at[dest]), w_up).astype(jnp.bfloat16)[None]
    )[0]
    fresh_mine = pick_blocks(every[0], later_at[me][None])
    saved_mine = pick_blocks(every[1], earlier_at[me][None])
    upstream_mine = pick_blocks(every[2], earlier_at[me][None])
    result = (fresh_mine.astype(jnp.float32) + mixed).astype(jnp.bfloat16)
    gradient = (
        upstream_mine.astype(jnp.float32) + norm_back(saved_mine, gain_row, returned)
    ).astype(jnp.bfloat16)
    arrive_forward = from_behind(result, "pipe", 1)
    arrive_backward = from_behind(gradient, "pipe", -1)
    return (arrive_forward[None, None], arrive_backward[None, None])


def solution(mesh):
    cores = 2
    shape = mesh.devices.shape
    fine = Mesh(
        mesh.devices.reshape(shape[0], shape[1], shape[2] // cores, cores),
        ("rep", "pipe", "zh", "core"),
    )
    rows = P("pipe", "rep", ("zh", "core"), None)
    in_specs = (
        rows,
        rows,
        rows,
        P("pipe", None),
        P("pipe", None, ("rep", "zh", "core")),
        P("pipe", ("rep", "zh", "core"), None),
        P(),
        P(),
        P(),
    )
    out_specs = (rows, rows)
    return jax.shard_map(local, mesh=fine, in_specs=in_specs, out_specs=out_specs, check_vma=False)
```

```python
import jax
import jax.numpy as jnp
from jax import lax
from jax.sharding import Mesh, PartitionSpec as P

BLOCK = 16
CAPB = 8
START = 5


EPSILON = 1e-05


def from_behind(block, axis, distance):
    devices = range(lax.axis_size(axis))
    route = [(i - distance, i) for i in devices if i - distance in devices]
    return lax.ppermute(block, axis, route)


def moved_blocks(counts, dests, replica_ids):
    return jnp.where((dests != replica_ids) & (counts > 0), counts, 0)


def section_plan(section_layers, redirect_count, redirect_dest, segments, replicas):
    replica_ids = jnp.arange(replicas, dtype=jnp.int32)
    section_ends = (jnp.cumsum(section_layers) - 1)[:-1]
    positions = jnp.arange(segments, dtype=jnp.int32)
    matches = (section_ends[None, :] == positions[:, None]).astype(jnp.int32)
    segment_count = jnp.sum(matches[:, :, None] * redirect_count[None, :, :], axis=1)
    has_boundary = jnp.sum(matches, axis=1)[:, None]
    segment_dest = (
        jnp.sum(matches[:, :, None] * redirect_dest[None, :, :], axis=1)
        + (1 - has_boundary) * replica_ids[None, :]
    )
    live_list = [jnp.full((replicas,), START, jnp.int32)]
    for position in range(segments - 1):
        moved = moved_blocks(segment_count[position], segment_dest[position], replica_ids)
        incoming = jnp.sum(
            jnp.where(segment_dest[position][:, None] == replica_ids[None, :], moved[:, None], 0),
            axis=0,
        )
        live_list.append(live_list[-1] - moved + incoming)
    return (jnp.stack(live_list), segment_count, segment_dest)


def source_rows(live_before, counts, dests, replicas):
    replica_ids = jnp.arange(replicas, dtype=jnp.int32)
    block_ids = jnp.arange(CAPB, dtype=jnp.int32)
    moved = moved_blocks(counts, dests, replica_ids)
    sends = moved > 0
    same_dest = (
        (dests[None, :] == dests[:, None])
        & (replica_ids[None, :] < replica_ids[:, None])
        & sends[None, :]
    )
    kept = live_before - moved
    incoming = jnp.sum(
        jnp.where(sends[:, None] & (dests[:, None] == replica_ids[None, :]), moved[:, None], 0),
        axis=0,
    )
    offset = jnp.sum(jnp.where(same_dest, moved[None, :], 0), axis=1)
    hits = (
        sends[None, None, :]
        & (dests[None, None, :] == replica_ids[:, None, None])
        & (block_ids[None, :, None] >= offset[None, None, :])
        & (block_ids[None, :, None] < (offset + moved)[None, None, :])
    )
    from_block = (
        replica_ids[None, None, :] * CAPB + block_ids[None, :, None] - offset[None, None, :]
    )
    moved_source = jnp.sum(jnp.where(hits, from_block, 0), axis=2)
    own_local = block_ids[None, :] - incoming[:, None]
    own_ok = (own_local >= 0) & (own_local < kept[:, None])
    own_block = own_local + moved[:, None]
    source_block = jnp.where(
        jnp.any(hits, axis=2),
        moved_source,
        jnp.where(own_ok, replica_ids[:, None] * CAPB + own_block, -1),
    )
    row_ids = source_block[:, :, None] * BLOCK + jnp.arange(BLOCK, dtype=jnp.int32)[None, None, :]
    return jnp.where(source_block[:, :, None] >= 0, row_ids, -1).reshape(replicas * CAPB * BLOCK)


def inverse_rows(source):
    total = source.shape[0]
    target = jnp.where(source >= 0, source, total)
    return (
        jnp.full((total,), -1, jnp.int32)
        .at[target]
        .set(jnp.arange(total, dtype=jnp.int32), mode="drop")
    )


def normalize(values, gain_row):
    wide = values.astype(jnp.float32)
    scale = lax.rsqrt(jnp.mean(wide * wide, axis=-1, keepdims=True) + EPSILON)
    return (wide * scale * gain_row.astype(jnp.float32)).astype(jnp.bfloat16)


def norm_back(values, gain_row, upstream):
    wide = values.astype(jnp.float32)
    scale = lax.rsqrt(jnp.mean(wide * wide, axis=-1, keepdims=True) + EPSILON)
    weighted = gain_row.astype(jnp.float32) * upstream
    return scale * weighted - wide * (scale * scale * scale) * jnp.mean(
        weighted * wide, axis=-1, keepdims=True
    )


def silu_slope(upper):
    sigma = jax.nn.sigmoid(upper)
    return sigma * (1.0 + upper * (1.0 - sigma))


def against_rows(left, right):
    return lax.dot_general(
        left, right, (((1,), (1,)), ((), ())), preferred_element_type=jnp.float32
    )


def pick_blocks(values, blocks):
    shaped = values.reshape(-1, BLOCK, values.shape[-1])
    taken = jnp.take(shaped, jnp.maximum(blocks, 0), axis=0)
    kept = jnp.where(blocks[:, None, None] >= 0, taken, jnp.zeros((), values.dtype))
    return kept.reshape(-1, values.shape[-1])


def row_blocks(rows):
    heads = rows[::BLOCK]
    return jnp.where(heads >= 0, heads // BLOCK, -1)


def swap_cores(values):
    return lax.ppermute(values, "core", [(0, 1), (1, 0)])


def gather_rows(values):
    group = lax.axis_size("rep") * lax.axis_size("zh")
    copies = jnp.broadcast_to(values[:, None], (values.shape[0], group) + values.shape[1:])
    near = lax.all_to_all(copies, ("rep", "zh"), 1, 1, tiled=True)
    both = jnp.stack([near, swap_cores(near)], axis=1)
    return both.reshape(values.shape[0], -1, values.shape[-1])


def scatter_rows(partial):
    width = partial.shape[-1]
    group = lax.axis_size("rep") * lax.axis_size("zh")
    shaped = partial.reshape(partial.shape[0], 2, group, BLOCK, width)
    total = shaped[:, 0].astype(jnp.float32) + swap_cores(shaped[:, 1]).astype(jnp.float32)
    parts = lax.all_to_all(total.astype(jnp.bfloat16), ("rep", "zh"), 1, 1, tiled=True)
    return jnp.sum(parts.astype(jnp.float32), axis=1)


def gathered_place(blocks, core_index):
    per_core, cores = lax.axis_size("zh"), lax.axis_size("core")
    split = blocks % (cores * per_core)
    spot = (split % cores != core_index) * (lax.axis_size("rep") * per_core)
    spot = spot + (blocks // (cores * per_core)) * per_core + split // cores
    return jnp.where(blocks >= 0, spot, -1)


def local(
    act_forward,
    act_saved,
    grad_output,
    norm_gain,
    up_weight,
    down_weight,
    section_layers,
    redirect_count,
    redirect_dest,
):
    segments = lax.axis_size("pipe")
    replicas = lax.axis_size("rep")
    per_core = lax.axis_size("zh")
    cores = lax.axis_size("core")
    segment_index = lax.axis_index("pipe")
    replica_index = lax.axis_index("rep")
    zh_index = lax.axis_index("zh")
    core_index = lax.axis_index("core")
    local_rows = act_forward.shape[2]
    gain_row = norm_gain[0]
    w_up = up_weight[0]
    w_down = down_weight[0]
    live, segment_count, segment_dest = section_plan(
        section_layers, redirect_count, redirect_dest, segments, replicas
    )
    prior = jnp.maximum(segment_index - 1, 0)
    later = row_blocks(
        source_rows(
            live[segment_index], segment_count[segment_index], segment_dest[segment_index], replicas
        )
    )
    earlier = row_blocks(
        inverse_rows(source_rows(live[prior], segment_count[prior], segment_dest[prior], replicas))
    )
    group = replicas * per_core
    slots = jnp.arange(cores * group, dtype=jnp.int32)
    slot_core = jnp.where(slots < group, core_index, cores - 1 - core_index)
    slot_group = slots % group
    dest = (slot_group // per_core) * (per_core * cores) + (slot_group % per_core) * cores + slot_core
    me = replica_index * (per_core * cores) + zh_index * cores + core_index
    later_at = gathered_place(later, core_index)
    earlier_at = gathered_place(earlier, core_index)
    fresh_every = gather_rows(act_forward[0])
    pair, fresh_every = lax.optimization_barrier(
        (jnp.stack([act_saved[0, 0], grad_output[0, 0]]), fresh_every)
    )
    saved_every, upstream_every = gather_rows(pair)
    every = (fresh_every[0], saved_every, upstream_every)
    hidden = jax.nn.silu(
        jnp.dot(normalize(every[0], gain_row), w_up, preferred_element_type=jnp.float32)
    ).astype(jnp.bfloat16)
    upper = jnp.dot(normalize(every[1], gain_row), w_up, preferred_element_type=jnp.float32)
    back_hidden = (against_rows(every[2], w_down) * silu_slope(upper)).astype(jnp.bfloat16)
    mixed = scatter_rows(
        jnp.dot(pick_blocks(hidden, later_at[dest]), w_down, preferred_element_type=jnp.float32).astype(
            jnp.bfloat16
        )[None]
    )[0]
    returned = scatter_rows(
        against_rows(pick_blocks(back_hidden, earlier_at[dest]), w_up).astype(jnp.bfloat16)[None]
    )[0]
    fresh_mine = pick_blocks(every[0], later_at[me][None])
    saved_mine = pick_blocks(every[1], earlier_at[me][None])
    upstream_mine = pick_blocks(every[2], earlier_at[me][None])
    result = (fresh_mine.astype(jnp.float32) + mixed).astype(jnp.bfloat16)
    gradient = (
        upstream_mine.astype(jnp.float32) + norm_back(saved_mine, gain_row, returned)
    ).astype(jnp.bfloat16)
    arrive_forward = from_behind(result, "pipe", 1)
    arrive_backward = from_behind(gradient, "pipe", -1)
    return (arrive_forward[None, None], arrive_backward[None, None])


def solution(mesh):
    cores = 2
    shape = mesh.devices.shape
    fine = Mesh(
        mesh.devices.reshape(shape[0], shape[1], shape[2] // cores, cores),
        ("rep", "pipe", "zh", "core"),
    )
    rows = P("pipe", "rep", ("zh", "core"), None)
    in_specs = (
        rows,
        rows,
        rows,
        P("pipe", None),
        P("pipe", None, ("rep", "zh", "core")),
        P("pipe", ("rep", "zh", "core"), None),
        P(),
        P(),
        P(),
    )
    out_specs = (rows, rows)
    return jax.shard_map(local, mesh=fine, in_specs=in_specs, out_specs=out_specs, check_vma=False)
```

```python
import jax
import jax.numpy as jnp
from jax import lax
from jax.sharding import Mesh, PartitionSpec as P

BLOCK = 16
CAPB = 8
START = 5


EPSILON = 1e-05


def from_behind(block, axis, distance):
    devices = range(lax.axis_size(axis))
    route = [(i - distance, i) for i in devices if i - distance in devices]
    return lax.ppermute(block, axis, route)


def moved_blocks(counts, dests, replica_ids):
    return jnp.where((dests != replica_ids) & (counts > 0), counts, 0)


def section_plan(section_layers, redirect_count, redirect_dest, segments, replicas):
    replica_ids = jnp.arange(replicas, dtype=jnp.int32)
    section_ends = (jnp.cumsum(section_layers) - 1)[:-1]
    positions = jnp.arange(segments, dtype=jnp.int32)
    matches = (section_ends[None, :] == positions[:, None]).astype(jnp.int32)
    segment_count = jnp.sum(matches[:, :, None] * redirect_count[None, :, :], axis=1)
    has_boundary = jnp.sum(matches, axis=1)[:, None]
    segment_dest = (
        jnp.sum(matches[:, :, None] * redirect_dest[None, :, :], axis=1)
        + (1 - has_boundary) * replica_ids[None, :]
    )
    live_list = [jnp.full((replicas,), START, jnp.int32)]
    for position in range(segments - 1):
        moved = moved_blocks(segment_count[position], segment_dest[position], replica_ids)
        incoming = jnp.sum(
            jnp.where(segment_dest[position][:, None] == replica_ids[None, :], moved[:, None], 0),
            axis=0,
        )
        live_list.append(live_list[-1] - moved + incoming)
    return (jnp.stack(live_list), segment_count, segment_dest)


def source_rows(live_before, counts, dests, replicas):
    replica_ids = jnp.arange(replicas, dtype=jnp.int32)
    block_ids = jnp.arange(CAPB, dtype=jnp.int32)
    moved = moved_blocks(counts, dests, replica_ids)
    sends = moved > 0
    same_dest = (
        (dests[None, :] == dests[:, None])
        & (replica_ids[None, :] < replica_ids[:, None])
        & sends[None, :]
    )
    kept = live_before - moved
    incoming = jnp.sum(
        jnp.where(sends[:, None] & (dests[:, None] == replica_ids[None, :]), moved[:, None], 0),
        axis=0,
    )
    offset = jnp.sum(jnp.where(same_dest, moved[None, :], 0), axis=1)
    hits = (
        sends[None, None, :]
        & (dests[None, None, :] == replica_ids[:, None, None])
        & (block_ids[None, :, None] >= offset[None, None, :])
        & (block_ids[None, :, None] < (offset + moved)[None, None, :])
    )
    from_block = (
        replica_ids[None, None, :] * CAPB + block_ids[None, :, None] - offset[None, None, :]
    )
    moved_source = jnp.sum(jnp.where(hits, from_block, 0), axis=2)
    own_local = block_ids[None, :] - incoming[:, None]
    own_ok = (own_local >= 0) & (own_local < kept[:, None])
    own_block = own_local + moved[:, None]
    source_block = jnp.where(
        jnp.any(hits, axis=2),
        moved_source,
        jnp.where(own_ok, replica_ids[:, None] * CAPB + own_block, -1),
    )
    row_ids = source_block[:, :, None] * BLOCK + jnp.arange(BLOCK, dtype=jnp.int32)[None, None, :]
    return jnp.where(source_block[:, :, None] >= 0, row_ids, -1).reshape(replicas * CAPB * BLOCK)


def inverse_rows(source):
    total = source.shape[0]
    target = jnp.where(source >= 0, source, total)
    return (
        jnp.full((total,), -1, jnp.int32)
        .at[target]
        .set(jnp.arange(total, dtype=jnp.int32), mode="drop")
    )


def normalize(values, gain_row):
    wide = values.astype(jnp.float32)
    scale = lax.rsqrt(jnp.mean(wide * wide, axis=-1, keepdims=True) + EPSILON)
    return (wide * scale * gain_row.astype(jnp.float32)).astype(jnp.bfloat16)


def norm_back(values, gain_row, upstream):
    wide = values.astype(jnp.float32)
    scale = lax.rsqrt(jnp.mean(wide * wide, axis=-1, keepdims=True) + EPSILON)
    weighted = gain_row.astype(jnp.float32) * upstream
    return scale * weighted - wide * (scale * scale * scale) * jnp.mean(
        weighted * wide, axis=-1, keepdims=True
    )


def silu_slope(upper):
    sigma = jax.nn.sigmoid(upper)
    return sigma * (1.0 + upper * (1.0 - sigma))


def against_rows(left, right):
    return lax.dot_general(
        left, right, (((1,), (1,)), ((), ())), preferred_element_type=jnp.float32
    )


def pick_blocks(values, blocks):
    shaped = values.reshape(-1, BLOCK, values.shape[-1])
    taken = jnp.take(shaped, jnp.maximum(blocks, 0), axis=0)
    kept = jnp.where(blocks[:, None, None] >= 0, taken, jnp.zeros((), values.dtype))
    return kept.reshape(-1, values.shape[-1])


def row_blocks(rows):
    heads = rows[::BLOCK]
    return jnp.where(heads >= 0, heads // BLOCK, -1)


def swap_cores(values):
    return lax.ppermute(values, "core", [(0, 1), (1, 0)])


def shift(values, axis, step):
    size = lax.axis_size(axis)
    return lax.ppermute(values, axis, [(i, (i + step) % size) for i in range(size)])


def ring_gather(values, axis):
    half = values.shape[-2] // 2
    from_left = shift(values, axis, 1)
    from_right = shift(values, axis, -1)
    first = shift(from_left[..., :half, :], axis, 1)
    second = shift(from_right[..., half:, :], axis, -1)
    far = jnp.concatenate([first, second], axis=-2)
    return jnp.stack([values, from_right, far, from_left])


def ring_scatter(parts, axis):
    half = parts.shape[-2] // 2
    far = parts[2].astype(jnp.bfloat16)
    from_left = shift(far[..., :half, :], axis, 1).astype(jnp.float32)
    from_right = shift(far[..., half:, :], axis, -1).astype(jnp.float32)
    up = jnp.concatenate([parts[1][..., :half, :] + from_left, parts[1][..., half:, :]], axis=-2)
    down = jnp.concatenate([parts[3][..., :half, :], parts[3][..., half:, :] + from_right], axis=-2)
    return (
        parts[0]
        + shift(up.astype(jnp.bfloat16), axis, 1).astype(jnp.float32)
        + shift(down.astype(jnp.bfloat16), axis, -1).astype(jnp.float32)
    )


def direct_gather(values, axis):
    return jnp.stack([values, shift(values, axis, -1), shift(values, axis, 2), shift(values, axis, 1)])


def direct_scatter(parts, axis):
    total = parts[0]
    for step in range(1, parts.shape[0]):
        total = total + shift(parts[step].astype(jnp.bfloat16), axis, step).astype(jnp.float32)
    return total


def gather_rows(values):
    near = ring_gather(direct_gather(values, "zh"), "rep")
    both = jnp.stack([near, swap_cores(near)])
    return both.reshape(-1, values.shape[-1])


def scatter_rows(partial):
    rows, width = BLOCK, partial.shape[-1]
    shaped = partial.reshape(2, lax.axis_size("rep"), lax.axis_size("zh"), rows, width)
    total = shaped[0].astype(jnp.float32) + swap_cores(shaped[1]).astype(jnp.float32)
    return direct_scatter(ring_scatter(total, "rep"), "zh")


def gathered_place(blocks, replica_index, zh_index, core_index):
    replicas, per_core, cores = lax.axis_size("rep"), lax.axis_size("zh"), lax.axis_size("core")
    split = blocks % (cores * per_core)
    spot = (split % cores != core_index) * (replicas * per_core)
    spot = spot + ((blocks // (cores * per_core) - replica_index) % replicas) * per_core
    spot = spot + (split // cores - zh_index) % per_core
    return jnp.where(blocks >= 0, spot, -1)


def local(
    act_forward,
    act_saved,
    grad_output,
    norm_gain,
    up_weight,
    down_weight,
    section_layers,
    redirect_count,
    redirect_dest,
):
    segments = lax.axis_size("pipe")
    replicas = lax.axis_size("rep")
    per_core = lax.axis_size("zh")
    cores = lax.axis_size("core")
    segment_index = lax.axis_index("pipe")
    replica_index = lax.axis_index("rep")
    zh_index = lax.axis_index("zh")
    core_index = lax.axis_index("core")
    local_rows = act_forward.shape[2]
    gain_row = norm_gain[0]
    w_up = up_weight[0]
    w_down = down_weight[0]
    live, segment_count, segment_dest = section_plan(
        section_layers, redirect_count, redirect_dest, segments, replicas
    )
    prior = jnp.maximum(segment_index - 1, 0)
    later = row_blocks(
        source_rows(
            live[segment_index], segment_count[segment_index], segment_dest[segment_index], replicas
        )
    )
    earlier = row_blocks(
        inverse_rows(source_rows(live[prior], segment_count[prior], segment_dest[prior], replicas))
    )
    group = replicas * per_core
    slots = jnp.arange(cores * group, dtype=jnp.int32)
    slot_core = jnp.where(slots < group, core_index, cores - 1 - core_index)
    slot_rep = (replica_index + (slots % group) // per_core) % replicas
    slot_zh = (zh_index + slots % per_core) % per_core
    dest = slot_rep * (per_core * cores) + slot_zh * cores + slot_core
    me = replica_index * (per_core * cores) + zh_index * cores + core_index
    later_at = gathered_place(later, replica_index, zh_index, core_index)
    earlier_at = gathered_place(earlier, replica_index, zh_index, core_index)
    every = [gather_rows(part[0, 0]) for part in (act_forward, act_saved, grad_output)]
    hidden = jax.nn.silu(
        jnp.dot(normalize(every[0], gain_row), w_up, preferred_element_type=jnp.float32)
    ).astype(jnp.bfloat16)
    upper = jnp.dot(normalize(every[1], gain_row), w_up, preferred_element_type=jnp.float32)
    back_hidden = (against_rows(every[2], w_down) * silu_slope(upper)).astype(jnp.bfloat16)
    mixed = scatter_rows(
        jnp.dot(pick_blocks(hidden, later_at[dest]), w_down, preferred_element_type=jnp.float32).astype(
            jnp.bfloat16
        )
    )
    returned = scatter_rows(
        against_rows(pick_blocks(back_hidden, earlier_at[dest]), w_up).astype(jnp.bfloat16)
    )
    fresh_mine = pick_blocks(every[0], later_at[me][None])
    saved_mine = pick_blocks(every[1], earlier_at[me][None])
    upstream_mine = pick_blocks(every[2], earlier_at[me][None])
    result = (fresh_mine.astype(jnp.float32) + mixed).astype(jnp.bfloat16)
    gradient = (
        upstream_mine.astype(jnp.float32) + norm_back(saved_mine, gain_row, returned)
    ).astype(jnp.bfloat16)
    arrive_forward = from_behind(result, "pipe", 1)
    arrive_backward = from_behind(gradient, "pipe", -1)
    return (arrive_forward[None, None], arrive_backward[None, None])


def solution(mesh):
    cores = 2
    shape = mesh.devices.shape
    fine = Mesh(
        mesh.devices.reshape(shape[0], shape[1], shape[2] // cores, cores),
        ("rep", "pipe", "zh", "core"),
    )
    rows = P("pipe", "rep", ("zh", "core"), None)
    in_specs = (
        rows,
        rows,
        rows,
        P("pipe", None),
        P("pipe", None, ("rep", "zh", "core")),
        P("pipe", ("rep", "zh", "core"), None),
        P(),
        P(),
        P(),
    )
    out_specs = (rows, rows)
    return jax.shard_map(local, mesh=fine, in_specs=in_specs, out_specs=out_specs, check_vma=False)
```

```python
import jax
import jax.numpy as jnp
from jax import lax
from jax.sharding import Mesh, PartitionSpec as P

BLOCK = 16
CAPB = 8
START = 5


EPSILON = 1e-05


def from_behind(block, axis, distance):
    devices = range(lax.axis_size(axis))
    route = [(i - distance, i) for i in devices if i - distance in devices]
    return lax.ppermute(block, axis, route)


def moved_blocks(counts, dests, replica_ids):
    return jnp.where((dests != replica_ids) & (counts > 0), counts, 0)


def section_plan(section_layers, redirect_count, redirect_dest, segments, replicas):
    replica_ids = jnp.arange(replicas, dtype=jnp.int32)
    section_ends = (jnp.cumsum(section_layers) - 1)[:-1]
    positions = jnp.arange(segments, dtype=jnp.int32)
    matches = (section_ends[None, :] == positions[:, None]).astype(jnp.int32)
    segment_count = jnp.sum(matches[:, :, None] * redirect_count[None, :, :], axis=1)
    has_boundary = jnp.sum(matches, axis=1)[:, None]
    segment_dest = (
        jnp.sum(matches[:, :, None] * redirect_dest[None, :, :], axis=1)
        + (1 - has_boundary) * replica_ids[None, :]
    )
    live_list = [jnp.full((replicas,), START, jnp.int32)]
    for position in range(segments - 1):
        moved = moved_blocks(segment_count[position], segment_dest[position], replica_ids)
        incoming = jnp.sum(
            jnp.where(segment_dest[position][:, None] == replica_ids[None, :], moved[:, None], 0),
            axis=0,
        )
        live_list.append(live_list[-1] - moved + incoming)
    return (jnp.stack(live_list), segment_count, segment_dest)


def source_rows(live_before, counts, dests, replicas):
    replica_ids = jnp.arange(replicas, dtype=jnp.int32)
    block_ids = jnp.arange(CAPB, dtype=jnp.int32)
    moved = moved_blocks(counts, dests, replica_ids)
    sends = moved > 0
    same_dest = (
        (dests[None, :] == dests[:, None])
        & (replica_ids[None, :] < replica_ids[:, None])
        & sends[None, :]
    )
    kept = live_before - moved
    incoming = jnp.sum(
        jnp.where(sends[:, None] & (dests[:, None] == replica_ids[None, :]), moved[:, None], 0),
        axis=0,
    )
    offset = jnp.sum(jnp.where(same_dest, moved[None, :], 0), axis=1)
    hits = (
        sends[None, None, :]
        & (dests[None, None, :] == replica_ids[:, None, None])
        & (block_ids[None, :, None] >= offset[None, None, :])
        & (block_ids[None, :, None] < (offset + moved)[None, None, :])
    )
    from_block = (
        replica_ids[None, None, :] * CAPB + block_ids[None, :, None] - offset[None, None, :]
    )
    moved_source = jnp.sum(jnp.where(hits, from_block, 0), axis=2)
    own_local = block_ids[None, :] - incoming[:, None]
    own_ok = (own_local >= 0) & (own_local < kept[:, None])
    own_block = own_local + moved[:, None]
    source_block = jnp.where(
        jnp.any(hits, axis=2),
        moved_source,
        jnp.where(own_ok, replica_ids[:, None] * CAPB + own_block, -1),
    )
    row_ids = source_block[:, :, None] * BLOCK + jnp.arange(BLOCK, dtype=jnp.int32)[None, None, :]
    return jnp.where(source_block[:, :, None] >= 0, row_ids, -1).reshape(replicas * CAPB * BLOCK)


def inverse_rows(source):
    total = source.shape[0]
    target = jnp.where(source >= 0, source, total)
    return (
        jnp.full((total,), -1, jnp.int32)
        .at[target]
        .set(jnp.arange(total, dtype=jnp.int32), mode="drop")
    )


def normalize(values, gain_row):
    wide = values.astype(jnp.float32)
    scale = lax.rsqrt(jnp.mean(wide * wide, axis=-1, keepdims=True) + EPSILON)
    return (wide * scale * gain_row.astype(jnp.float32)).astype(jnp.bfloat16)


def norm_back(values, gain_row, upstream):
    wide = values.astype(jnp.float32)
    scale = lax.rsqrt(jnp.mean(wide * wide, axis=-1, keepdims=True) + EPSILON)
    weighted = gain_row.astype(jnp.float32) * upstream
    return scale * weighted - wide * (scale * scale * scale) * jnp.mean(
        weighted * wide, axis=-1, keepdims=True
    )


def silu_slope(upper):
    sigma = jax.nn.sigmoid(upper)
    return sigma * (1.0 + upper * (1.0 - sigma))


def against_rows(left, right):
    return lax.dot_general(
        left, right, (((1,), (1,)), ((), ())), preferred_element_type=jnp.float32
    )


def pick_blocks(values, blocks):
    shaped = values.reshape(-1, BLOCK, values.shape[-1])
    taken = jnp.take(shaped, jnp.maximum(blocks, 0), axis=0)
    kept = jnp.where(blocks[:, None, None] >= 0, taken, jnp.zeros((), values.dtype))
    return kept.reshape(-1, values.shape[-1])


def row_blocks(rows):
    heads = rows[::BLOCK]
    return jnp.where(heads >= 0, heads // BLOCK, -1)


def swap_cores(values):
    return lax.ppermute(values, "core", [(0, 1), (1, 0)])


def shift(values, axis, step):
    size = lax.axis_size(axis)
    return lax.ppermute(values, axis, [(i, (i + step) % size) for i in range(size)])


def ring_gather(values, axis):
    half = values.shape[-2] // 2
    from_left = shift(values, axis, 1)
    from_right = shift(values, axis, -1)
    first = shift(from_left[..., :half, :], axis, 1)
    second = shift(from_right[..., half:, :], axis, -1)
    far = jnp.concatenate([first, second], axis=-2)
    return jnp.stack([values, from_right, far, from_left])


def ring_scatter(parts, axis):
    half = parts.shape[-2] // 2
    far = parts[2].astype(jnp.bfloat16)
    from_left = shift(far[..., :half, :], axis, 1).astype(jnp.float32)
    from_right = shift(far[..., half:, :], axis, -1).astype(jnp.float32)
    up = jnp.concatenate([parts[1][..., :half, :] + from_left, parts[1][..., half:, :]], axis=-2)
    down = jnp.concatenate([parts[3][..., :half, :], parts[3][..., half:, :] + from_right], axis=-2)
    return (
        parts[0]
        + shift(up.astype(jnp.bfloat16), axis, 1).astype(jnp.float32)
        + shift(down.astype(jnp.bfloat16), axis, -1).astype(jnp.float32)
    )


def direct_gather(values, axis):
    return jnp.stack([values, shift(values, axis, -1), shift(values, axis, 2), shift(values, axis, 1)])


def direct_scatter(parts, axis):
    total = parts[0]
    for step in range(1, parts.shape[0]):
        total = total + shift(parts[step].astype(jnp.bfloat16), axis, step).astype(jnp.float32)
    return total


def gather_rows(values):
    near = ring_gather(direct_gather(values, "zh"), "rep")
    both = jnp.stack([near, swap_cores(near)])
    return both.reshape(-1, values.shape[-1])


def scatter_rows(partial):
    rows, width = BLOCK, partial.shape[-1]
    shaped = partial.reshape(2, lax.axis_size("rep"), lax.axis_size("zh"), rows, width)
    total = shaped[0].astype(jnp.float32) + swap_cores(shaped[1]).astype(jnp.float32)
    return direct_scatter(direct_scatter(total, "rep"), "zh")


def gathered_place(blocks, replica_index, zh_index, core_index):
    replicas, per_core, cores = lax.axis_size("rep"), lax.axis_size("zh"), lax.axis_size("core")
    split = blocks % (cores * per_core)
    spot = (split % cores != core_index) * (replicas * per_core)
    spot = spot + ((blocks // (cores * per_core) - replica_index) % replicas) * per_core
    spot = spot + (split // cores - zh_index) % per_core
    return jnp.where(blocks >= 0, spot, -1)


def local(
    act_forward,
    act_saved,
    grad_output,
    norm_gain,
    up_weight,
    down_weight,
    section_layers,
    redirect_count,
    redirect_dest,
):
    segments = lax.axis_size("pipe")
    replicas = lax.axis_size("rep")
    per_core = lax.axis_size("zh")
    cores = lax.axis_size("core")
    segment_index = lax.axis_index("pipe")
    replica_index = lax.axis_index("rep")
    zh_index = lax.axis_index("zh")
    core_index = lax.axis_index("core")
    local_rows = act_forward.shape[2]
    gain_row = norm_gain[0]
    w_up = up_weight[0]
    w_down = down_weight[0]
    live, segment_count, segment_dest = section_plan(
        section_layers, redirect_count, redirect_dest, segments, replicas
    )
    prior = jnp.maximum(segment_index - 1, 0)
    later = row_blocks(
        source_rows(
            live[segment_index], segment_count[segment_index], segment_dest[segment_index], replicas
        )
    )
    earlier = row_blocks(
        inverse_rows(source_rows(live[prior], segment_count[prior], segment_dest[prior], replicas))
    )
    group = replicas * per_core
    slots = jnp.arange(cores * group, dtype=jnp.int32)
    slot_core = jnp.where(slots < group, core_index, cores - 1 - core_index)
    slot_rep = (replica_index + (slots % group) // per_core) % replicas
    slot_zh = (zh_index + slots % per_core) % per_core
    dest = slot_rep * (per_core * cores) + slot_zh * cores + slot_core
    me = replica_index * (per_core * cores) + zh_index * cores + core_index
    later_at = gathered_place(later, replica_index, zh_index, core_index)
    earlier_at = gathered_place(earlier, replica_index, zh_index, core_index)
    every = [gather_rows(part[0, 0]) for part in (act_forward, act_saved, grad_output)]
    hidden = jax.nn.silu(
        jnp.dot(normalize(every[0], gain_row), w_up, preferred_element_type=jnp.float32)
    ).astype(jnp.bfloat16)
    upper = jnp.dot(normalize(every[1], gain_row), w_up, preferred_element_type=jnp.float32)
    back_hidden = (against_rows(every[2], w_down) * silu_slope(upper)).astype(jnp.bfloat16)
    mixed = scatter_rows(
        jnp.dot(pick_blocks(hidden, later_at[dest]), w_down, preferred_element_type=jnp.float32).astype(
            jnp.bfloat16
        )
    )
    returned = scatter_rows(
        against_rows(pick_blocks(back_hidden, earlier_at[dest]), w_up).astype(jnp.bfloat16)
    )
    fresh_mine = pick_blocks(every[0], later_at[me][None])
    saved_mine = pick_blocks(every[1], earlier_at[me][None])
    upstream_mine = pick_blocks(every[2], earlier_at[me][None])
    result = (fresh_mine.astype(jnp.float32) + mixed).astype(jnp.bfloat16)
    gradient = (
        upstream_mine.astype(jnp.float32) + norm_back(saved_mine, gain_row, returned)
    ).astype(jnp.bfloat16)
    arrive_forward = from_behind(result, "pipe", 1)
    arrive_backward = from_behind(gradient, "pipe", -1)
    return (arrive_forward[None, None], arrive_backward[None, None])


def solution(mesh):
    cores = 2
    shape = mesh.devices.shape
    fine = Mesh(
        mesh.devices.reshape(shape[0], shape[1], shape[2] // cores, cores),
        ("rep", "pipe", "zh", "core"),
    )
    rows = P("pipe", "rep", ("zh", "core"), None)
    in_specs = (
        rows,
        rows,
        rows,
        P("pipe", None),
        P("pipe", None, ("rep", "zh", "core")),
        P("pipe", ("rep", "zh", "core"), None),
        P(),
        P(),
        P(),
    )
    out_specs = (rows, rows)
    return jax.shard_map(local, mesh=fine, in_specs=in_specs, out_specs=out_specs, check_vma=False)
```

```python
import jax
import jax.numpy as jnp
from jax import lax
from jax.sharding import Mesh, PartitionSpec as P

BLOCK = 16
CAPB = 8
START = 5


EPSILON = 1e-05


def from_behind(block, axis, distance):
    devices = range(lax.axis_size(axis))
    route = [(i - distance, i) for i in devices if i - distance in devices]
    return lax.ppermute(block, axis, route)


def moved_blocks(counts, dests, replica_ids):
    return jnp.where((dests != replica_ids) & (counts > 0), counts, 0)


def section_plan(section_layers, redirect_count, redirect_dest, segments, replicas):
    replica_ids = jnp.arange(replicas, dtype=jnp.int32)
    section_ends = (jnp.cumsum(section_layers) - 1)[:-1]
    positions = jnp.arange(segments, dtype=jnp.int32)
    matches = (section_ends[None, :] == positions[:, None]).astype(jnp.int32)
    segment_count = jnp.sum(matches[:, :, None] * redirect_count[None, :, :], axis=1)
    has_boundary = jnp.sum(matches, axis=1)[:, None]
    segment_dest = (
        jnp.sum(matches[:, :, None] * redirect_dest[None, :, :], axis=1)
        + (1 - has_boundary) * replica_ids[None, :]
    )
    live_list = [jnp.full((replicas,), START, jnp.int32)]
    for position in range(segments - 1):
        moved = moved_blocks(segment_count[position], segment_dest[position], replica_ids)
        incoming = jnp.sum(
            jnp.where(segment_dest[position][:, None] == replica_ids[None, :], moved[:, None], 0),
            axis=0,
        )
        live_list.append(live_list[-1] - moved + incoming)
    return (jnp.stack(live_list), segment_count, segment_dest)


def source_rows(live_before, counts, dests, replicas):
    replica_ids = jnp.arange(replicas, dtype=jnp.int32)
    block_ids = jnp.arange(CAPB, dtype=jnp.int32)
    moved = moved_blocks(counts, dests, replica_ids)
    sends = moved > 0
    same_dest = (
        (dests[None, :] == dests[:, None])
        & (replica_ids[None, :] < replica_ids[:, None])
        & sends[None, :]
    )
    kept = live_before - moved
    incoming = jnp.sum(
        jnp.where(sends[:, None] & (dests[:, None] == replica_ids[None, :]), moved[:, None], 0),
        axis=0,
    )
    offset = jnp.sum(jnp.where(same_dest, moved[None, :], 0), axis=1)
    hits = (
        sends[None, None, :]
        & (dests[None, None, :] == replica_ids[:, None, None])
        & (block_ids[None, :, None] >= offset[None, None, :])
        & (block_ids[None, :, None] < (offset + moved)[None, None, :])
    )
    from_block = (
        replica_ids[None, None, :] * CAPB + block_ids[None, :, None] - offset[None, None, :]
    )
    moved_source = jnp.sum(jnp.where(hits, from_block, 0), axis=2)
    own_local = block_ids[None, :] - incoming[:, None]
    own_ok = (own_local >= 0) & (own_local < kept[:, None])
    own_block = own_local + moved[:, None]
    source_block = jnp.where(
        jnp.any(hits, axis=2),
        moved_source,
        jnp.where(own_ok, replica_ids[:, None] * CAPB + own_block, -1),
    )
    row_ids = source_block[:, :, None] * BLOCK + jnp.arange(BLOCK, dtype=jnp.int32)[None, None, :]
    return jnp.where(source_block[:, :, None] >= 0, row_ids, -1).reshape(replicas * CAPB * BLOCK)


def inverse_rows(source):
    total = source.shape[0]
    target = jnp.where(source >= 0, source, total)
    return (
        jnp.full((total,), -1, jnp.int32)
        .at[target]
        .set(jnp.arange(total, dtype=jnp.int32), mode="drop")
    )


def normalize(values, gain_row):
    wide = values.astype(jnp.float32)
    scale = lax.rsqrt(jnp.mean(wide * wide, axis=-1, keepdims=True) + EPSILON)
    return (wide * scale * gain_row.astype(jnp.float32)).astype(jnp.bfloat16)


def norm_back(values, gain_row, upstream):
    wide = values.astype(jnp.float32)
    scale = lax.rsqrt(jnp.mean(wide * wide, axis=-1, keepdims=True) + EPSILON)
    weighted = gain_row.astype(jnp.float32) * upstream
    return scale * weighted - wide * (scale * scale * scale) * jnp.mean(
        weighted * wide, axis=-1, keepdims=True
    )


def silu_slope(upper):
    sigma = jax.nn.sigmoid(upper)
    return sigma * (1.0 + upper * (1.0 - sigma))


def against_rows(left, right):
    return lax.dot_general(
        left, right, (((1,), (1,)), ((), ())), preferred_element_type=jnp.float32
    )


def pick_blocks(values, blocks):
    shaped = values.reshape(-1, BLOCK, values.shape[-1])
    taken = jnp.take(shaped, jnp.maximum(blocks, 0), axis=0)
    kept = jnp.where(blocks[:, None, None] >= 0, taken, jnp.zeros((), values.dtype))
    return kept.reshape(-1, values.shape[-1])


def row_blocks(rows):
    heads = rows[::BLOCK]
    return jnp.where(heads >= 0, heads // BLOCK, -1)


def swap_cores(values):
    return lax.ppermute(values, "core", [(0, 1), (1, 0)])


def shift(values, axis, step):
    size = lax.axis_size(axis)
    return lax.ppermute(values, axis, [(i, (i + step) % size) for i in range(size)])


def ring_gather(values, axis):
    half = values.shape[-2] // 2
    from_left = shift(values, axis, 1)
    from_right = shift(values, axis, -1)
    first = shift(from_left[..., :half, :], axis, 1)
    second = shift(from_right[..., half:, :], axis, -1)
    far = jnp.concatenate([first, second], axis=-2)
    return jnp.stack([values, from_right, far, from_left])


def ring_scatter(parts, axis):
    half = parts.shape[-2] // 2
    far = parts[2].astype(jnp.bfloat16)
    from_left = shift(far[..., :half, :], axis, 1).astype(jnp.float32)
    from_right = shift(far[..., half:, :], axis, -1).astype(jnp.float32)
    up = jnp.concatenate([parts[1][..., :half, :] + from_left, parts[1][..., half:, :]], axis=-2)
    down = jnp.concatenate([parts[3][..., :half, :], parts[3][..., half:, :] + from_right], axis=-2)
    return (
        parts[0]
        + shift(up.astype(jnp.bfloat16), axis, 1).astype(jnp.float32)
        + shift(down.astype(jnp.bfloat16), axis, -1).astype(jnp.float32)
    )


def direct_gather(values, axis):
    return jnp.stack([values, shift(values, axis, -1), shift(values, axis, 2), shift(values, axis, 1)])


def direct_scatter(parts, axis):
    total = parts[0]
    for step in range(1, parts.shape[0]):
        total = total + shift(parts[step].astype(jnp.bfloat16), axis, step).astype(jnp.float32)
    return total


def gather_rows(values):
    near = ring_gather(direct_gather(values, "zh"), "rep")
    both = jnp.stack([near, swap_cores(near)])
    return both.reshape(-1, values.shape[-1])


def scatter_rows(partial):
    rows, width = BLOCK, partial.shape[-1]
    shaped = partial.reshape(2, lax.axis_size("rep"), lax.axis_size("zh"), rows, width)
    total = shaped[0].astype(jnp.float32) + swap_cores(shaped[1]).astype(jnp.float32)
    return direct_scatter(ring_scatter(total, "rep"), "zh")


def gathered_place(blocks, replica_index, zh_index, core_index):
    replicas, per_core, cores = lax.axis_size("rep"), lax.axis_size("zh"), lax.axis_size("core")
    split = blocks % (cores * per_core)
    spot = (split % cores != core_index) * (replicas * per_core)
    spot = spot + ((blocks // (cores * per_core) - replica_index) % replicas) * per_core
    spot = spot + (split // cores - zh_index) % per_core
    return jnp.where(blocks >= 0, spot, -1)


def local(
    act_forward,
    act_saved,
    grad_output,
    norm_gain,
    up_weight,
    down_weight,
    section_layers,
    redirect_count,
    redirect_dest,
):
    segments = lax.axis_size("pipe")
    replicas = lax.axis_size("rep")
    per_core = lax.axis_size("zh")
    cores = lax.axis_size("core")
    segment_index = lax.axis_index("pipe")
    replica_index = lax.axis_index("rep")
    zh_index = lax.axis_index("zh")
    core_index = lax.axis_index("core")
    local_rows = act_forward.shape[2]
    gain_row = norm_gain[0]
    w_up = up_weight[0]
    w_down = down_weight[0]
    live, segment_count, segment_dest = section_plan(
        section_layers, redirect_count, redirect_dest, segments, replicas
    )
    prior = jnp.maximum(segment_index - 1, 0)
    later = row_blocks(
        source_rows(
            live[segment_index], segment_count[segment_index], segment_dest[segment_index], replicas
        )
    )
    earlier = row_blocks(
        inverse_rows(source_rows(live[prior], segment_count[prior], segment_dest[prior], replicas))
    )
    group = replicas * per_core
    slots = jnp.arange(cores * group, dtype=jnp.int32)
    slot_core = jnp.where(slots < group, core_index, cores - 1 - core_index)
    slot_rep = (replica_index + (slots % group) // per_core) % replicas
    slot_zh = (zh_index + slots % per_core) % per_core
    dest = slot_rep * (per_core * cores) + slot_zh * cores + slot_core
    me = replica_index * (per_core * cores) + zh_index * cores + core_index
    later_at = gathered_place(later, replica_index, zh_index, core_index)
    earlier_at = gathered_place(earlier, replica_index, zh_index, core_index)
    saved_every = gather_rows(act_saved[0, 0])
    upstream_every = gather_rows(grad_output[0, 0])
    fresh_own, saved_every, upstream_every = lax.optimization_barrier(
        (act_forward[0, 0], saved_every, upstream_every)
    )
    every = [gather_rows(fresh_own), saved_every, upstream_every]
    hidden = jax.nn.silu(
        jnp.dot(normalize(every[0], gain_row), w_up, preferred_element_type=jnp.float32)
    ).astype(jnp.bfloat16)
    upper = jnp.dot(normalize(every[1], gain_row), w_up, preferred_element_type=jnp.float32)
    back_hidden = (against_rows(every[2], w_down) * silu_slope(upper)).astype(jnp.bfloat16)
    mixed = scatter_rows(
        jnp.dot(pick_blocks(hidden, later_at[dest]), w_down, preferred_element_type=jnp.float32).astype(
            jnp.bfloat16
        )
    )
    returned = scatter_rows(
        against_rows(pick_blocks(back_hidden, earlier_at[dest]), w_up).astype(jnp.bfloat16)
    )
    fresh_mine = pick_blocks(every[0], later_at[me][None])
    saved_mine = pick_blocks(every[1], earlier_at[me][None])
    upstream_mine = pick_blocks(every[2], earlier_at[me][None])
    result = (fresh_mine.astype(jnp.float32) + mixed).astype(jnp.bfloat16)
    gradient = (
        upstream_mine.astype(jnp.float32) + norm_back(saved_mine, gain_row, returned)
    ).astype(jnp.bfloat16)
    arrive_forward = from_behind(result, "pipe", 1)
    arrive_backward = from_behind(gradient, "pipe", -1)
    return (arrive_forward[None, None], arrive_backward[None, None])


def solution(mesh):
    cores = 2
    shape = mesh.devices.shape
    fine = Mesh(
        mesh.devices.reshape(shape[0], shape[1], shape[2] // cores, cores),
        ("rep", "pipe", "zh", "core"),
    )
    rows = P("pipe", "rep", ("zh", "core"), None)
    in_specs = (
        rows,
        rows,
        rows,
        P("pipe", None),
        P("pipe", None, ("rep", "zh", "core")),
        P("pipe", ("rep", "zh", "core"), None),
        P(),
        P(),
        P(),
    )
    out_specs = (rows, rows)
    return jax.shard_map(local, mesh=fine, in_specs=in_specs, out_specs=out_specs, check_vma=False)
```

```python
import jax
import jax.numpy as jnp
from jax import lax
from jax.sharding import Mesh, PartitionSpec as P

BLOCK = 16
CAPB = 8
START = 5


EPSILON = 1e-05


def from_behind(block, axis, distance):
    devices = range(lax.axis_size(axis))
    route = [(i - distance, i) for i in devices if i - distance in devices]
    return lax.ppermute(block, axis, route)


def moved_blocks(counts, dests, replica_ids):
    return jnp.where((dests != replica_ids) & (counts > 0), counts, 0)


def section_plan(section_layers, redirect_count, redirect_dest, segments, replicas):
    replica_ids = jnp.arange(replicas, dtype=jnp.int32)
    section_ends = (jnp.cumsum(section_layers) - 1)[:-1]
    positions = jnp.arange(segments, dtype=jnp.int32)
    matches = (section_ends[None, :] == positions[:, None]).astype(jnp.int32)
    segment_count = jnp.sum(matches[:, :, None] * redirect_count[None, :, :], axis=1)
    has_boundary = jnp.sum(matches, axis=1)[:, None]
    segment_dest = (
        jnp.sum(matches[:, :, None] * redirect_dest[None, :, :], axis=1)
        + (1 - has_boundary) * replica_ids[None, :]
    )
    live_list = [jnp.full((replicas,), START, jnp.int32)]
    for position in range(segments - 1):
        moved = moved_blocks(segment_count[position], segment_dest[position], replica_ids)
        incoming = jnp.sum(
            jnp.where(segment_dest[position][:, None] == replica_ids[None, :], moved[:, None], 0),
            axis=0,
        )
        live_list.append(live_list[-1] - moved + incoming)
    return (jnp.stack(live_list), segment_count, segment_dest)


def source_rows(live_before, counts, dests, replicas):
    replica_ids = jnp.arange(replicas, dtype=jnp.int32)
    block_ids = jnp.arange(CAPB, dtype=jnp.int32)
    moved = moved_blocks(counts, dests, replica_ids)
    sends = moved > 0
    same_dest = (
        (dests[None, :] == dests[:, None])
        & (replica_ids[None, :] < replica_ids[:, None])
        & sends[None, :]
    )
    kept = live_before - moved
    incoming = jnp.sum(
        jnp.where(sends[:, None] & (dests[:, None] == replica_ids[None, :]), moved[:, None], 0),
        axis=0,
    )
    offset = jnp.sum(jnp.where(same_dest, moved[None, :], 0), axis=1)
    hits = (
        sends[None, None, :]
        & (dests[None, None, :] == replica_ids[:, None, None])
        & (block_ids[None, :, None] >= offset[None, None, :])
        & (block_ids[None, :, None] < (offset + moved)[None, None, :])
    )
    from_block = (
        replica_ids[None, None, :] * CAPB + block_ids[None, :, None] - offset[None, None, :]
    )
    moved_source = jnp.sum(jnp.where(hits, from_block, 0), axis=2)
    own_local = block_ids[None, :] - incoming[:, None]
    own_ok = (own_local >= 0) & (own_local < kept[:, None])
    own_block = own_local + moved[:, None]
    source_block = jnp.where(
        jnp.any(hits, axis=2),
        moved_source,
        jnp.where(own_ok, replica_ids[:, None] * CAPB + own_block, -1),
    )
    row_ids = source_block[:, :, None] * BLOCK + jnp.arange(BLOCK, dtype=jnp.int32)[None, None, :]
    return jnp.where(source_block[:, :, None] >= 0, row_ids, -1).reshape(replicas * CAPB * BLOCK)


def inverse_rows(source):
    total = source.shape[0]
    target = jnp.where(source >= 0, source, total)
    return (
        jnp.full((total,), -1, jnp.int32)
        .at[target]
        .set(jnp.arange(total, dtype=jnp.int32), mode="drop")
    )


def normalize(values, gain_row):
    wide = values.astype(jnp.float32)
    scale = lax.rsqrt(jnp.mean(wide * wide, axis=-1, keepdims=True) + EPSILON)
    return (wide * scale * gain_row.astype(jnp.float32)).astype(jnp.bfloat16)


def norm_back(values, gain_row, upstream):
    wide = values.astype(jnp.float32)
    scale = lax.rsqrt(jnp.mean(wide * wide, axis=-1, keepdims=True) + EPSILON)
    weighted = gain_row.astype(jnp.float32) * upstream
    return scale * weighted - wide * (scale * scale * scale) * jnp.mean(
        weighted * wide, axis=-1, keepdims=True
    )


def silu_slope(upper):
    sigma = jax.nn.sigmoid(upper)
    return sigma * (1.0 + upper * (1.0 - sigma))


def against_rows(left, right):
    return lax.dot_general(
        left, right, (((1,), (1,)), ((), ())), preferred_element_type=jnp.float32
    )


def pick_blocks(values, blocks):
    shaped = values.reshape(-1, BLOCK, values.shape[-1])
    taken = jnp.take(shaped, jnp.maximum(blocks, 0), axis=0)
    kept = jnp.where(blocks[:, None, None] >= 0, taken, jnp.zeros((), values.dtype))
    return kept.reshape(-1, values.shape[-1])


def row_blocks(rows):
    heads = rows[::BLOCK]
    return jnp.where(heads >= 0, heads // BLOCK, -1)


def swap_cores(values):
    return lax.ppermute(values, "core", [(0, 1), (1, 0)])


def shift(values, axis, step):
    size = lax.axis_size(axis)
    return lax.ppermute(values, axis, [(i, (i + step) % size) for i in range(size)])


def ring_gather(values, axis):
    half = values.shape[-2] // 2
    from_left = shift(values, axis, 1)
    from_right = shift(values, axis, -1)
    first = shift(from_left[..., :half, :], axis, 1)
    second = shift(from_right[..., half:, :], axis, -1)
    far = jnp.concatenate([first, second], axis=-2)
    return jnp.stack([values, from_right, far, from_left])


def ring_scatter(parts, axis):
    half = parts.shape[-2] // 2
    far = parts[2].astype(jnp.bfloat16)
    from_left = shift(far[..., :half, :], axis, 1).astype(jnp.float32)
    from_right = shift(far[..., half:, :], axis, -1).astype(jnp.float32)
    up = jnp.concatenate([parts[1][..., :half, :] + from_left, parts[1][..., half:, :]], axis=-2)
    down = jnp.concatenate([parts[3][..., :half, :], parts[3][..., half:, :] + from_right], axis=-2)
    return (
        parts[0]
        + shift(up.astype(jnp.bfloat16), axis, 1).astype(jnp.float32)
        + shift(down.astype(jnp.bfloat16), axis, -1).astype(jnp.float32)
    )


def direct_gather(values, axis):
    return jnp.stack([values, shift(values, axis, -1), shift(values, axis, 2), shift(values, axis, 1)])


def direct_scatter(parts, axis):
    total = parts[0]
    for step in range(1, parts.shape[0]):
        total = total + shift(parts[step].astype(jnp.bfloat16), axis, step).astype(jnp.float32)
    return total


def gather_rows(values):
    near = ring_gather(direct_gather(values, "zh"), "rep")
    both = jnp.stack([near, swap_cores(near)])
    return both.reshape(-1, values.shape[-1])


def scatter_rows(partial):
    rows, width = BLOCK, partial.shape[-1]
    shaped = partial.reshape(2, lax.axis_size("rep"), lax.axis_size("zh"), rows, width)
    total = shaped[0].astype(jnp.float32) + swap_cores(shaped[1]).astype(jnp.float32)
    return direct_scatter(ring_scatter(total, "rep"), "zh")


def gathered_place(blocks, replica_index, zh_index, core_index):
    replicas, per_core, cores = lax.axis_size("rep"), lax.axis_size("zh"), lax.axis_size("core")
    split = blocks % (cores * per_core)
    spot = (split % cores != core_index) * (replicas * per_core)
    spot = spot + ((blocks // (cores * per_core) - replica_index) % replicas) * per_core
    spot = spot + (split // cores - zh_index) % per_core
    return jnp.where(blocks >= 0, spot, -1)


def local(
    act_forward,
    act_saved,
    grad_output,
    norm_gain,
    up_weight,
    down_weight,
    section_layers,
    redirect_count,
    redirect_dest,
):
    segments = lax.axis_size("pipe")
    replicas = lax.axis_size("rep")
    per_core = lax.axis_size("zh")
    cores = lax.axis_size("core")
    segment_index = lax.axis_index("pipe")
    replica_index = lax.axis_index("rep")
    zh_index = lax.axis_index("zh")
    core_index = lax.axis_index("core")
    local_rows = act_forward.shape[2]
    gain_row = norm_gain[0]
    w_up = up_weight[0]
    w_down = down_weight[0]
    live, segment_count, segment_dest = section_plan(
        section_layers, redirect_count, redirect_dest, segments, replicas
    )
    prior = jnp.maximum(segment_index - 1, 0)
    later = row_blocks(
        source_rows(
            live[segment_index], segment_count[segment_index], segment_dest[segment_index], replicas
        )
    )
    earlier = row_blocks(
        inverse_rows(source_rows(live[prior], segment_count[prior], segment_dest[prior], replicas))
    )
    group = replicas * per_core
    slots = jnp.arange(cores * group, dtype=jnp.int32)
    slot_core = jnp.where(slots < group, core_index, cores - 1 - core_index)
    slot_rep = (replica_index + (slots % group) // per_core) % replicas
    slot_zh = (zh_index + slots % per_core) % per_core
    dest = slot_rep * (per_core * cores) + slot_zh * cores + slot_core
    me = replica_index * (per_core * cores) + zh_index * cores + core_index
    later_at = gathered_place(later, replica_index, zh_index, core_index)
    earlier_at = gathered_place(earlier, replica_index, zh_index, core_index)
    fresh_every = gather_rows(act_forward[0, 0])
    saved_own, upstream_own, fresh_every = lax.optimization_barrier(
        (act_saved[0, 0], grad_output[0, 0], fresh_every)
    )
    every = [fresh_every, gather_rows(saved_own), gather_rows(upstream_own)]
    hidden = jax.nn.silu(
        jnp.dot(normalize(every[0], gain_row), w_up, preferred_element_type=jnp.float32)
    ).astype(jnp.bfloat16)
    upper = jnp.dot(normalize(every[1], gain_row), w_up, preferred_element_type=jnp.float32)
    back_hidden = (against_rows(every[2], w_down) * silu_slope(upper)).astype(jnp.bfloat16)
    mixed = scatter_rows(
        jnp.dot(pick_blocks(hidden, later_at[dest]), w_down, preferred_element_type=jnp.float32).astype(
            jnp.bfloat16
        )
    )
    returned = scatter_rows(
        against_rows(pick_blocks(back_hidden, earlier_at[dest]), w_up).astype(jnp.bfloat16)
    )
    fresh_mine = pick_blocks(every[0], later_at[me][None])
    saved_mine = pick_blocks(every[1], earlier_at[me][None])
    upstream_mine = pick_blocks(every[2], earlier_at[me][None])
    result = (fresh_mine.astype(jnp.float32) + mixed).astype(jnp.bfloat16)
    gradient = (
        upstream_mine.astype(jnp.float32) + norm_back(saved_mine, gain_row, returned)
    ).astype(jnp.bfloat16)
    arrive_forward = from_behind(result, "pipe", 1)
    arrive_backward = from_behind(gradient, "pipe", -1)
    return (arrive_forward[None, None], arrive_backward[None, None])


def solution(mesh):
    cores = 2
    shape = mesh.devices.shape
    fine = Mesh(
        mesh.devices.reshape(shape[0], shape[1], shape[2] // cores, cores),
        ("rep", "pipe", "zh", "core"),
    )
    rows = P("pipe", "rep", ("zh", "core"), None)
    in_specs = (
        rows,
        rows,
        rows,
        P("pipe", None),
        P("pipe", None, ("rep", "zh", "core")),
        P("pipe", ("rep", "zh", "core"), None),
        P(),
        P(),
        P(),
    )
    out_specs = (rows, rows)
    return jax.shard_map(local, mesh=fine, in_specs=in_specs, out_specs=out_specs, check_vma=False)
```

```python
import jax
import jax.numpy as jnp
from jax import lax
from jax.sharding import Mesh, PartitionSpec as P

BLOCK = 16
CAPB = 8
START = 5


EPSILON = 1e-05


def from_behind(block, axis, distance):
    devices = range(lax.axis_size(axis))
    route = [(i - distance, i) for i in devices if i - distance in devices]
    return lax.ppermute(block, axis, route)


def moved_blocks(counts, dests, replica_ids):
    return jnp.where((dests != replica_ids) & (counts > 0), counts, 0)


def section_plan(section_layers, redirect_count, redirect_dest, segments, replicas):
    replica_ids = jnp.arange(replicas, dtype=jnp.int32)
    section_ends = (jnp.cumsum(section_layers) - 1)[:-1]
    positions = jnp.arange(segments, dtype=jnp.int32)
    matches = (section_ends[None, :] == positions[:, None]).astype(jnp.int32)
    segment_count = jnp.sum(matches[:, :, None] * redirect_count[None, :, :], axis=1)
    has_boundary = jnp.sum(matches, axis=1)[:, None]
    segment_dest = (
        jnp.sum(matches[:, :, None] * redirect_dest[None, :, :], axis=1)
        + (1 - has_boundary) * replica_ids[None, :]
    )
    live_list = [jnp.full((replicas,), START, jnp.int32)]
    for position in range(segments - 1):
        moved = moved_blocks(segment_count[position], segment_dest[position], replica_ids)
        incoming = jnp.sum(
            jnp.where(segment_dest[position][:, None] == replica_ids[None, :], moved[:, None], 0),
            axis=0,
        )
        live_list.append(live_list[-1] - moved + incoming)
    return (jnp.stack(live_list), segment_count, segment_dest)


def source_rows(live_before, counts, dests, replicas):
    replica_ids = jnp.arange(replicas, dtype=jnp.int32)
    block_ids = jnp.arange(CAPB, dtype=jnp.int32)
    moved = moved_blocks(counts, dests, replica_ids)
    sends = moved > 0
    same_dest = (
        (dests[None, :] == dests[:, None])
        & (replica_ids[None, :] < replica_ids[:, None])
        & sends[None, :]
    )
    kept = live_before - moved
    incoming = jnp.sum(
        jnp.where(sends[:, None] & (dests[:, None] == replica_ids[None, :]), moved[:, None], 0),
        axis=0,
    )
    offset = jnp.sum(jnp.where(same_dest, moved[None, :], 0), axis=1)
    hits = (
        sends[None, None, :]
        & (dests[None, None, :] == replica_ids[:, None, None])
        & (block_ids[None, :, None] >= offset[None, None, :])
        & (block_ids[None, :, None] < (offset + moved)[None, None, :])
    )
    from_block = (
        replica_ids[None, None, :] * CAPB + block_ids[None, :, None] - offset[None, None, :]
    )
    moved_source = jnp.sum(jnp.where(hits, from_block, 0), axis=2)
    own_local = block_ids[None, :] - incoming[:, None]
    own_ok = (own_local >= 0) & (own_local < kept[:, None])
    own_block = own_local + moved[:, None]
    source_block = jnp.where(
        jnp.any(hits, axis=2),
        moved_source,
        jnp.where(own_ok, replica_ids[:, None] * CAPB + own_block, -1),
    )
    row_ids = source_block[:, :, None] * BLOCK + jnp.arange(BLOCK, dtype=jnp.int32)[None, None, :]
    return jnp.where(source_block[:, :, None] >= 0, row_ids, -1).reshape(replicas * CAPB * BLOCK)


def inverse_rows(source):
    total = source.shape[0]
    target = jnp.where(source >= 0, source, total)
    return (
        jnp.full((total,), -1, jnp.int32)
        .at[target]
        .set(jnp.arange(total, dtype=jnp.int32), mode="drop")
    )


def normalize(values, gain_row):
    wide = values.astype(jnp.float32)
    scale = lax.rsqrt(jnp.mean(wide * wide, axis=-1, keepdims=True) + EPSILON)
    return (wide * scale * gain_row.astype(jnp.float32)).astype(jnp.bfloat16)


def norm_back(values, gain_row, upstream):
    wide = values.astype(jnp.float32)
    scale = lax.rsqrt(jnp.mean(wide * wide, axis=-1, keepdims=True) + EPSILON)
    weighted = gain_row.astype(jnp.float32) * upstream
    return scale * weighted - wide * (scale * scale * scale) * jnp.mean(
        weighted * wide, axis=-1, keepdims=True
    )


def silu_slope(upper):
    sigma = jax.nn.sigmoid(upper)
    return sigma * (1.0 + upper * (1.0 - sigma))


def against_rows(left, right):
    return lax.dot_general(
        left, right, (((1,), (1,)), ((), ())), preferred_element_type=jnp.float32
    )


def pick_blocks(values, blocks):
    shaped = values.reshape(-1, BLOCK, values.shape[-1])
    taken = jnp.take(shaped, jnp.maximum(blocks, 0), axis=0)
    kept = jnp.where(blocks[:, None, None] >= 0, taken, jnp.zeros((), values.dtype))
    return kept.reshape(-1, values.shape[-1])


def row_blocks(rows):
    heads = rows[::BLOCK]
    return jnp.where(heads >= 0, heads // BLOCK, -1)


def swap_cores(values):
    return lax.ppermute(values, "core", [(0, 1), (1, 0)])


def shift(values, axis, step):
    size = lax.axis_size(axis)
    return lax.ppermute(values, axis, [(i, (i + step) % size) for i in range(size)])


def ring_gather(values, axis):
    half = values.shape[-2] // 2
    from_left = shift(values, axis, 1)
    from_right = shift(values, axis, -1)
    first = shift(from_left[..., :half, :], axis, 1)
    second = shift(from_right[..., half:, :], axis, -1)
    far = jnp.concatenate([first, second], axis=-2)
    return jnp.stack([values, from_right, far, from_left])


def ring_scatter(parts, axis):
    half = parts.shape[-2] // 2
    far = parts[2].astype(jnp.bfloat16)
    from_left = shift(far[..., :half, :], axis, 1).astype(jnp.float32)
    from_right = shift(far[..., half:, :], axis, -1).astype(jnp.float32)
    up = jnp.concatenate([parts[1][..., :half, :] + from_left, parts[1][..., half:, :]], axis=-2)
    down = jnp.concatenate([parts[3][..., :half, :], parts[3][..., half:, :] + from_right], axis=-2)
    return (
        parts[0]
        + shift(up.astype(jnp.bfloat16), axis, 1).astype(jnp.float32)
        + shift(down.astype(jnp.bfloat16), axis, -1).astype(jnp.float32)
    )


def direct_gather(values, axis):
    return jnp.stack([values, shift(values, axis, -1), shift(values, axis, 2), shift(values, axis, 1)])


def direct_scatter(parts, axis):
    total = parts[0]
    for step in range(1, parts.shape[0]):
        total = total + shift(parts[step].astype(jnp.bfloat16), axis, step).astype(jnp.float32)
    return total


def gather_rows(values, spread=ring_gather):
    near = spread(direct_gather(values, "zh"), "rep")
    both = jnp.stack([near, swap_cores(near)])
    return both.reshape(-1, values.shape[-1])


def scatter_rows(partial):
    rows, width = BLOCK, partial.shape[-1]
    shaped = partial.reshape(2, lax.axis_size("rep"), lax.axis_size("zh"), rows, width)
    total = shaped[0].astype(jnp.float32) + swap_cores(shaped[1]).astype(jnp.float32)
    return direct_scatter(ring_scatter(total, "rep"), "zh")


def gathered_place(blocks, replica_index, zh_index, core_index):
    replicas, per_core, cores = lax.axis_size("rep"), lax.axis_size("zh"), lax.axis_size("core")
    split = blocks % (cores * per_core)
    spot = (split % cores != core_index) * (replicas * per_core)
    spot = spot + ((blocks // (cores * per_core) - replica_index) % replicas) * per_core
    spot = spot + (split // cores - zh_index) % per_core
    return jnp.where(blocks >= 0, spot, -1)


def local(
    act_forward,
    act_saved,
    grad_output,
    norm_gain,
    up_weight,
    down_weight,
    section_layers,
    redirect_count,
    redirect_dest,
):
    segments = lax.axis_size("pipe")
    replicas = lax.axis_size("rep")
    per_core = lax.axis_size("zh")
    cores = lax.axis_size("core")
    segment_index = lax.axis_index("pipe")
    replica_index = lax.axis_index("rep")
    zh_index = lax.axis_index("zh")
    core_index = lax.axis_index("core")
    local_rows = act_forward.shape[2]
    gain_row = norm_gain[0]
    w_up = up_weight[0]
    w_down = down_weight[0]
    live, segment_count, segment_dest = section_plan(
        section_layers, redirect_count, redirect_dest, segments, replicas
    )
    prior = jnp.maximum(segment_index - 1, 0)
    later = row_blocks(
        source_rows(
            live[segment_index], segment_count[segment_index], segment_dest[segment_index], replicas
        )
    )
    earlier = row_blocks(
        inverse_rows(source_rows(live[prior], segment_count[prior], segment_dest[prior], replicas))
    )
    group = replicas * per_core
    slots = jnp.arange(cores * group, dtype=jnp.int32)
    slot_core = jnp.where(slots < group, core_index, cores - 1 - core_index)
    slot_rep = (replica_index + (slots % group) // per_core) % replicas
    slot_zh = (zh_index + slots % per_core) % per_core
    dest = slot_rep * (per_core * cores) + slot_zh * cores + slot_core
    me = replica_index * (per_core * cores) + zh_index * cores + core_index
    later_at = gathered_place(later, replica_index, zh_index, core_index)
    earlier_at = gathered_place(earlier, replica_index, zh_index, core_index)
    every = [
        gather_rows(act_forward[0, 0], direct_gather),
        gather_rows(act_saved[0, 0]),
        gather_rows(grad_output[0, 0]),
    ]
    hidden = jax.nn.silu(
        jnp.dot(normalize(every[0], gain_row), w_up, preferred_element_type=jnp.float32)
    ).astype(jnp.bfloat16)
    upper = jnp.dot(normalize(every[1], gain_row), w_up, preferred_element_type=jnp.float32)
    back_hidden = (against_rows(every[2], w_down) * silu_slope(upper)).astype(jnp.bfloat16)
    mixed = scatter_rows(
        jnp.dot(pick_blocks(hidden, later_at[dest]), w_down, preferred_element_type=jnp.float32).astype(
            jnp.bfloat16
        )
    )
    returned = scatter_rows(
        against_rows(pick_blocks(back_hidden, earlier_at[dest]), w_up).astype(jnp.bfloat16)
    )
    fresh_mine = pick_blocks(every[0], later_at[me][None])
    saved_mine = pick_blocks(every[1], earlier_at[me][None])
    upstream_mine = pick_blocks(every[2], earlier_at[me][None])
    result = (fresh_mine.astype(jnp.float32) + mixed).astype(jnp.bfloat16)
    gradient = (
        upstream_mine.astype(jnp.float32) + norm_back(saved_mine, gain_row, returned)
    ).astype(jnp.bfloat16)
    arrive_forward = from_behind(result, "pipe", 1)
    arrive_backward = from_behind(gradient, "pipe", -1)
    return (arrive_forward[None, None], arrive_backward[None, None])


def solution(mesh):
    cores = 2
    shape = mesh.devices.shape
    fine = Mesh(
        mesh.devices.reshape(shape[0], shape[1], shape[2] // cores, cores),
        ("rep", "pipe", "zh", "core"),
    )
    rows = P("pipe", "rep", ("zh", "core"), None)
    in_specs = (
        rows,
        rows,
        rows,
        P("pipe", None),
        P("pipe", None, ("rep", "zh", "core")),
        P("pipe", ("rep", "zh", "core"), None),
        P(),
        P(),
        P(),
    )
    out_specs = (rows, rows)
    return jax.shard_map(local, mesh=fine, in_specs=in_specs, out_specs=out_specs, check_vma=False)
```
